32 devices in a mesh: layer: 8 (over z, x), feat: 4 (over y, core).
Axes of the slice: x: 2, y: 2, z: 4, core: 2. Of those that a mesh axis runs over, the one named last changes fastest.
Arguments:
- resid: bfloat16 [8, 128, 2304], P('layer', None, 'feat'), may hold values from -6 to 6
- encoder: bfloat16 [8, 2304, 4096], P('layer', None, 'feat'), may hold values from -0.125 to 0.125
- encoder_bias: float32 [8, 4096], P('layer', 'feat'), may hold values from -3 to 3
- decoder: bfloat16 [8, 4, 4096, 2304], P('layer', None, 'feat'), may hold values from -0.5 to 0.5
- decoder_bias: float32 [4, 2304], P(None, 'feat'), may hold values from -3 to 3
- topk_index: int32 [4, 256, 64], replicated, may hold values from 0 to 8191, all different within a row
- target: bfloat16 [4, 256, 2304], P(None, 'layer', 'feat'), may hold values from -6 to 6
Outputs:
- recon_error: bfloat16 [4, 256, 2304], P(None, 'layer', 'feat')
- grad_resid: bfloat16 [8, 128, 2304], P('layer', None, 'feat')
The draws below stay inside these ranges and needn't reach their ends.
Inputs may be any that keep to these rules, and one draw needn't show every extreme that they name: `topk_index`: each row names 64 distinct features of its layer, and every feature is named by some row of some layer.
All inputs are finite; a program needn't handle non-finite values.
Results may differ from the reference program's by a relative error of at most 0.0058.
Values may be sent and summed in bfloat16 or wider, within the bound.
No kernel may reach another device: no remote copies, remote signals or barrier semaphores. Data moves between devices by JAX's collectives and lax.ppermute only.
A program may use at most 128 MiB of HBM per device.

```python
import jax
import jax.numpy as jnp
from jax import lax

D = 2304
FEAT = 8192
TOPK = 64
TOKENS = 256
LAYERS = 4


def block_levels(rng, extent, cuts, low, largest):
    gain = 1.0
    for axis_at, parts in cuts:
        steps = jax.random.uniform(jax.random.fold_in(jax.random.fold_in(rng, 6), axis_at), (parts,), jnp.float32, low / len(cuts), largest / len(cuts))
        gain = gain * jnp.repeat(jnp.exp(steps), extent[axis_at] // parts).reshape((-1,) + (1,) * (len(extent) - 1 - axis_at))
    return gain


def different_ones(rng, rows, amount, top, lift):
    ranking = jax.random.permutation(jax.random.fold_in(rng, 1), amount)
    pull = ranking
    for power in range(3):
        pull = pull * pull // amount
    pull = pull * lift // amount
    lots = jax.random.randint(jax.random.fold_in(rng, 2), (rows, amount), 0, 4096) + pull
    holders = jax.random.permutation(jax.random.fold_in(rng, 3), rows)[jnp.arange(amount) % rows]
    lots = jnp.where(jnp.arange(rows)[:, None] == holders[None, :], 1 << 14, lots)
    priority = lots * amount + jnp.arange(amount)
    return lax.top_k(priority.astype(jnp.int32), top)[1].astype(jnp.int32)


def noise(stream_key, shape, scale, most, pieces=(), held_as=jnp.bfloat16):
    factor_of = block_levels(stream_key, shape, pieces, -0.22, 0.18) if pieces else 1.0
    array = jax.random.normal(stream_key, shape, jnp.float32) * scale * factor_of
    return jnp.minimum(jnp.maximum(array, -most), most).astype(held_as)


def setup_inputs(seed: int = 0) -> dict:
    arg_keys = jax.random.split(jax.random.key(seed), 8)
    return {
        "resid": noise(arg_keys[0], (2 * LAYERS, TOKENS // 2, D), 1.0, 6.0, ((0, 8), (2, 4))),
        "encoder": noise(arg_keys[1], (2 * LAYERS, D, FEAT // 2), D ** -0.5, 0.125, ((0, 8), (2, 4))),
        "encoder_bias": noise(arg_keys[2], (2 * LAYERS, FEAT // 2), 0.5, 3.0, ((0, 8), (1, 4)), jnp.float32),
        "decoder": noise(arg_keys[3], (2 * LAYERS, LAYERS, FEAT // 2, D), (TOPK * LAYERS // 2) ** -0.5, 0.5, ((0, 8), (2, 4))),
        "decoder_bias": noise(arg_keys[4], (LAYERS, D), 0.5, 3.0, ((1, 4),), jnp.float32),
        "topk_index": different_ones(arg_keys[5], LAYERS * TOKENS, FEAT, TOPK, 64).reshape((LAYERS, TOKENS, TOPK)),
        "target": noise(arg_keys[6], (LAYERS, TOKENS, D), 1.0, 6.0, ((1, 8), (2, 4))),
    }


def reference(resid, encoder, encoder_bias, decoder, decoder_bias, topk_index, target):
    masks = []
    weights = []
    acts = []
    for layer in range(LAYERS):
        tokens_all = jnp.concatenate([resid[2 * layer], resid[2 * layer + 1]], axis=0)
        weight = jnp.concatenate([encoder[2 * layer], encoder[2 * layer + 1]], axis=1)
        bias = jnp.concatenate([encoder_bias[2 * layer], encoder_bias[2 * layer + 1]])
        pre = jnp.dot(tokens_all, weight, preferred_element_type=jnp.float32) + bias
        row_ids = jnp.arange(TOKENS, dtype=jnp.int32)[:, None]
        mask = jnp.zeros((TOKENS, FEAT), jnp.float32).at[row_ids, topk_index[layer]].set(1.0)
        masks.append(mask)
        weights.append(weight)
        acts.append((mask * pre).astype(jnp.bfloat16))

    def decoder_rows(source, dest_layer):
        return jnp.concatenate([decoder[2 * source, dest_layer], decoder[2 * source + 1, dest_layer]], axis=0)

    errors = []
    for dest_layer in range(LAYERS):
        total = jnp.zeros((TOKENS, D), jnp.float32) + decoder_bias[dest_layer]
        for source in range(dest_layer + 1):
            total = total + jnp.dot(acts[source], decoder_rows(source, dest_layer), preferred_element_type=jnp.float32)
        errors.append((total - target[dest_layer].astype(jnp.float32)).astype(jnp.bfloat16))

    grads = []
    for source in range(LAYERS):
        grad_act = jnp.zeros((TOKENS, FEAT), jnp.float32)
        for dest_layer in range(source, LAYERS):
            grad_act = grad_act + jnp.dot(errors[dest_layer], decoder_rows(source, dest_layer).T, preferred_element_type=jnp.float32)
        grad_pre = (masks[source] * grad_act).astype(jnp.bfloat16)
        grad_in = jnp.dot(grad_pre, weights[source].T, preferred_element_type=jnp.float32).astype(jnp.bfloat16)
        grads.append(grad_in[: TOKENS // 2])
        grads.append(grad_in[TOKENS // 2:])
    return jnp.stack(errors), jnp.stack(grads)
```

```python
import jax
import jax.numpy as jnp
from jax import lax
from jax.sharding import Mesh
from jax.sharding import PartitionSpec as P

PLANE = ("lx", "feat")
EVERY = ("lz", "lx", "feat")


def local(resid, encoder, encoder_bias, decoder, decoder_bias, topk_index, target):
    planes = lax.axis_size("lz")
    feat_parts = lax.axis_size("feat")
    layer_id = lax.axis_index("lz")
    half_bit = lax.axis_index("lx")
    feat_pos = lax.axis_index("feat")
    layer_count = decoder.shape[1]
    feat_dev = encoder.shape[2]
    half_rows = resid.shape[1]
    cols = resid.shape[2]
    tokens = 2 * half_rows
    width = cols * feat_parts
    slots = 2 * planes
    slot_rows = tokens // slots
    feat_total = 2 * feat_parts * feat_dev

    gathered = lax.all_gather(resid[0], PLANE, axis=0, tiled=False)
    tokens_all = (
        gathered.reshape(2, feat_parts, half_rows, cols).transpose(0, 2, 1, 3).reshape(tokens, width)
    )
    pre = jnp.dot(tokens_all, encoder[0], preferred_element_type=jnp.float32) + encoder_bias[0]
    first_feat = half_bit * (feat_total // 2) + feat_pos * feat_dev
    feat_ids = first_feat + lax.iota(jnp.int32, feat_dev)
    layer_index = lax.dynamic_index_in_dim(topk_index, layer_id, 0, keepdims=False)
    selected = jnp.any(layer_index[:, :, None] == feat_ids[None, None, :], axis=1).astype(
        jnp.float32
    )
    acts = (selected * pre).astype(jnp.bfloat16)
    live_layers = lax.iota(jnp.int32, layer_count) >= layer_id
    partial_value = jnp.einsum("tf,lfd->ltd", acts, decoder[0], preferred_element_type=jnp.float32)
    partial_value = jnp.where(live_layers[:, None, None], partial_value, 0.0)
    blocks = (
        partial_value.reshape(layer_count, slots, slot_rows, feat_parts, cols)
        .transpose(1, 3, 0, 2, 4)
        .reshape(slots * feat_parts, layer_count, slot_rows, cols)
    )
    recon = lax.psum_scatter(blocks, EVERY, scatter_dimension=0, tiled=True)[0]
    recon = recon + decoder_bias[:, None, :]
    error = (recon - target.astype(jnp.float32)).astype(jnp.bfloat16)
    pieces = lax.all_gather(error, EVERY, axis=0, tiled=False)
    piece = (
        pieces.reshape(slots, feat_parts, layer_count, slot_rows, cols)
        .transpose(2, 0, 3, 1, 4)
        .reshape(layer_count, tokens, width)
    )
    kept = jnp.where(live_layers[:, None, None], piece, jnp.zeros_like(piece))
    grad_act = jnp.einsum("ltd,lfd->tf", kept, decoder[0], preferred_element_type=jnp.float32)
    grad_pre = (selected * grad_act).astype(jnp.bfloat16)
    grad_part = lax.dot_general(
        grad_pre, encoder[0], (((1,), (1,)), ((), ())), preferred_element_type=jnp.float32
    )
    grad_blocks = (
        grad_part.reshape(2, half_rows, feat_parts, cols)
        .transpose(0, 2, 1, 3)
        .reshape(2 * feat_parts, half_rows, cols)
    )
    grad_sum = lax.psum_scatter(grad_blocks, PLANE, scatter_dimension=0, tiled=True)
    return (error, grad_sum.astype(jnp.bfloat16))


def solution(mesh):
    layer_n = mesh.shape["layer"]
    feat_n = mesh.shape["feat"]
    split = Mesh(mesh.devices.reshape(layer_n // 2, 2, feat_n), ("lz", "lx", "feat"))
    slot = ("lz", "lx")
    in_specs = (
        P(slot, None, "feat"),
        P(slot, None, "feat"),
        P(slot, "feat"),
        P(slot, None, "feat", None),
        P(None, "feat"),
        P(),
        P(None, slot, "feat"),
    )
    out_specs = (P(None, slot, "feat"), P(slot, None, "feat"))
    return jax.shard_map(local, mesh=split, in_specs=in_specs, out_specs=out_specs, check_vma=False)
```

```python
import jax
import jax.numpy as jnp
from jax import lax
from jax.sharding import Mesh
from jax.sharding import PartitionSpec as P

PLANE = ("lx", "feat")
EVERY = ("lz", "lx", "feat")


def local(resid, encoder, encoder_bias, decoder, decoder_bias, topk_index, target):
    planes = lax.axis_size("lz")
    feat_parts = lax.axis_size("feat")
    layer_id = lax.axis_index("lz")
    half_bit = lax.axis_index("lx")
    feat_pos = lax.axis_index("feat")
    layer_count = decoder.shape[1]
    feat_dev = encoder.shape[2]
    half_rows = resid.shape[1]
    cols = resid.shape[2]
    tokens = 2 * half_rows
    width = cols * feat_parts
    slots = 2 * planes
    slot_rows = tokens // slots
    feat_total = 2 * feat_parts * feat_dev

    gathered = lax.all_gather(resid[0], PLANE, axis=0, tiled=False)
    tokens_all = (
        gathered.reshape(2, feat_parts, half_rows, cols).transpose(0, 2, 1, 3).reshape(tokens, width)
    )
    pre = jnp.dot(tokens_all, encoder[0], preferred_element_type=jnp.float32) + encoder_bias[0]
    first_feat = half_bit * (feat_total // 2) + feat_pos * feat_dev
    feat_ids = first_feat + lax.iota(jnp.int32, feat_dev)
    layer_index = lax.dynamic_index_in_dim(topk_index, layer_id, 0, keepdims=False)
    selected = jnp.any(layer_index[:, :, None] == feat_ids[None, None, :], axis=1).astype(
        jnp.float32
    )
    acts = (selected * pre).astype(jnp.bfloat16)
    live_layers = lax.iota(jnp.int32, layer_count) >= layer_id
    partial_value = jnp.einsum("tf,lfd->ltd", acts, decoder[0], preferred_element_type=jnp.float32)
    partial_value = jnp.where(live_layers[:, None, None], partial_value, 0.0)
    blocks = (
        partial_value.reshape(layer_count, slots, slot_rows, feat_parts, cols)
        .transpose(1, 3, 0, 2, 4)
        .reshape(slots * feat_parts, layer_count, slot_rows, cols)
    )
    recon = lax.psum_scatter(blocks.astype(jnp.bfloat16), EVERY, scatter_dimension=0, tiled=True)[0]
    recon = recon.astype(jnp.float32) + decoder_bias[:, None, :]
    error = (recon - target.astype(jnp.float32)).astype(jnp.bfloat16)
    pieces = lax.all_gather(error, EVERY, axis=0, tiled=False)
    piece = (
        pieces.reshape(slots, feat_parts, layer_count, slot_rows, cols)
        .transpose(2, 0, 3, 1, 4)
        .reshape(layer_count, tokens, width)
    )
    kept = jnp.where(live_layers[:, None, None], piece, jnp.zeros_like(piece))
    grad_act = jnp.einsum("ltd,lfd->tf", kept, decoder[0], preferred_element_type=jnp.float32)
    grad_pre = (selected * grad_act).astype(jnp.bfloat16)
    grad_part = lax.dot_general(
        grad_pre, encoder[0], (((1,), (1,)), ((), ())), preferred_element_type=jnp.float32
    )
    grad_blocks = (
        grad_part.reshape(2, half_rows, feat_parts, cols)
        .transpose(0, 2, 1, 3)
        .reshape(2 * feat_parts, half_rows, cols)
    )
    grad_sum = lax.psum_scatter(grad_blocks.astype(jnp.bfloat16), PLANE, scatter_dimension=0, tiled=True)
    return (error, grad_sum.astype(jnp.bfloat16))


def solution(mesh):
    layer_n = mesh.shape["layer"]
    feat_n = mesh.shape["feat"]
    split = Mesh(mesh.devices.reshape(layer_n // 2, 2, feat_n), ("lz", "lx", "feat"))
    slot = ("lz", "lx")
    in_specs = (
        P(slot, None, "feat"),
        P(slot, None, "feat"),
        P(slot, "feat"),
        P(slot, None, "feat", None),
        P(None, "feat"),
        P(),
        P(None, slot, "feat"),
    )
    out_specs = (P(None, slot, "feat"), P(slot, None, "feat"))
    return jax.shard_map(local, mesh=split, in_specs=in_specs, out_specs=out_specs, check_vma=False)
```

```python
import jax
import jax.numpy as jnp
from jax import lax
from jax.sharding import Mesh
from jax.sharding import PartitionSpec as P

PLANE = ("lx", "feat")
EVERY = ("lz", "lx", "feat")


def bit_labels(axes):
    labels = []
    for axis in axes:
        size = lax.axis_size(axis)
        bits = size.bit_length() - 1
        assert 1 << bits == size
        labels += [(axis, b) for b in reversed(range(bits))]
    return labels


def plan(axes):
    labels = bit_labels(axes)
    prefix = [("feat", 0)]
    suffix = [("lz", lax.axis_size("lz").bit_length() - 2)] if "lz" in axes else []
    rotation = [label for label in labels if label not in prefix + suffix]
    orders = [rotation[p:] + rotation[:p] for p in range(len(rotation))]
    return labels, prefix, orders, suffix


def row_split(rows, parts):
    base = (rows // (8 * parts)) * 8
    sizes = [base] * parts
    extra = rows - base * parts
    i = 0
    while extra >= 8:
        sizes[i % parts] += 8
        extra -= 8
        i += 1
    sizes[0] += extra
    return sizes


def partner(axis, bit):
    return [(i, i ^ (1 << bit)) for i in range(lax.axis_size(axis))]


def halve(x, labels, label):
    axis, bit = label
    dim = labels.index(label)
    own = (lax.axis_index(axis) >> bit) & 1
    keep = lax.dynamic_index_in_dim(x, own, dim, keepdims=False)
    send = lax.dynamic_index_in_dim(x, 1 - own, dim, keepdims=False)
    recv = lax.ppermute(send, axis, partner(axis, bit))
    return keep + recv, [l for l in labels if l != label]


def double(x, labels, label):
    axis, bit = label
    own = (lax.axis_index(axis) >> bit) & 1
    recv = lax.ppermute(x, axis, partner(axis, bit))
    low = jnp.where(own == 0, x, recv)
    high = jnp.where(own == 0, recv, x)
    return jnp.stack([low, high]), [label] + labels


def reduce_scatter(blocks, axes):
    labels, prefix, orders, suffix = plan(axes)
    n, rows, cols = blocks.shape
    x = blocks.reshape([2] * len(labels) + [rows, cols])
    cur = list(labels)
    for label in prefix:
        x, cur = halve(x, cur, label)
    sizes = row_split(rows, len(orders))
    starts = [sum(sizes[:i]) for i in range(len(sizes))]
    parts = [lax.slice_in_dim(x, s, s + z, axis=x.ndim - 2) for s, z in zip(starts, sizes)]
    curs = [list(cur) for _ in parts]
    for step in range(len(orders[0]) + len(suffix)):
        for p in range(len(parts)):
            label = (orders[p] + suffix)[step]
            parts[p], curs[p] = halve(parts[p], curs[p], label)
    return jnp.concatenate(parts, axis=0)


def all_gather(block, axes):
    labels, prefix, orders, suffix = plan(axes)
    rows, cols = block.shape
    sizes = row_split(rows, len(orders))
    starts = [sum(sizes[:i]) for i in range(len(sizes))]
    parts = [lax.slice_in_dim(block, s, s + z, axis=0) for s, z in zip(starts, sizes)]
    curs = [[] for _ in parts]
    for step in range(len(orders[0]) + len(suffix)):
        for p in range(len(parts)):
            label = list(reversed(orders[p] + suffix))[step]
            parts[p], curs[p] = double(parts[p], curs[p], label)
    cur = curs[0]
    parts = [jnp.transpose(x, [c.index(l) for l in cur] + [x.ndim - 2, x.ndim - 1]) for x, c in zip(parts, curs)]
    x = jnp.concatenate(parts, axis=-2)
    for label in reversed(prefix):
        x, cur = double(x, cur, label)
    x = jnp.transpose(x, [cur.index(l) for l in labels] + [x.ndim - 2, x.ndim - 1])
    return x.reshape(-1, rows, cols)


def local(resid, encoder, encoder_bias, decoder, decoder_bias, topk_index, target):
    planes = lax.axis_size("lz")
    feat_parts = lax.axis_size("feat")
    layer_id = lax.axis_index("lz")
    half_bit = lax.axis_index("lx")
    feat_pos = lax.axis_index("feat")
    layer_count = decoder.shape[1]
    feat_dev = encoder.shape[2]
    half_rows = resid.shape[1]
    cols = resid.shape[2]
    tokens = 2 * half_rows
    width = cols * feat_parts
    slots = 2 * planes
    slot_rows = tokens // slots
    feat_total = 2 * feat_parts * feat_dev

    gathered = all_gather(resid[0], PLANE)
    tokens_all = (
        gathered.reshape(2, feat_parts, half_rows, cols).transpose(0, 2, 1, 3).reshape(tokens, width)
    )
    pre = jnp.dot(tokens_all, encoder[0], preferred_element_type=jnp.float32) + encoder_bias[0]
    first_feat = half_bit * (feat_total // 2) + feat_pos * feat_dev
    feat_ids = first_feat + lax.iota(jnp.int32, feat_dev)
    layer_index = lax.dynamic_index_in_dim(topk_index, layer_id, 0, keepdims=False)
    selected = jnp.any(layer_index[:, :, None] == feat_ids[None, None, :], axis=1).astype(
        jnp.float32
    )
    acts = (selected * pre).astype(jnp.bfloat16)
    live_layers = lax.iota(jnp.int32, layer_count) >= layer_id
    partial_value = jnp.einsum("tf,lfd->ltd", acts, decoder[0], preferred_element_type=jnp.float32)
    partial_value = jnp.where(live_layers[:, None, None], partial_value, 0.0)
    blocks = (
        partial_value.reshape(layer_count, slots, slot_rows, feat_parts, cols)
        .transpose(1, 3, 0, 2, 4)
        .reshape(slots * feat_parts, layer_count * slot_rows, cols)
    )
    recon = reduce_scatter(blocks, EVERY).reshape(layer_count, slot_rows, cols)
    recon = recon + decoder_bias[:, None, :]
    error = (recon - target.astype(jnp.float32)).astype(jnp.bfloat16)
    pieces = all_gather(error.reshape(layer_count * slot_rows, cols), EVERY)
    piece = (
        pieces.reshape(slots, feat_parts, layer_count, slot_rows, cols)
        .transpose(2, 0, 3, 1, 4)
        .reshape(layer_count, tokens, width)
    )
    kept = jnp.where(live_layers[:, None, None], piece, jnp.zeros_like(piece))
    grad_act = jnp.einsum("ltd,lfd->tf", kept, decoder[0], preferred_element_type=jnp.float32)
    grad_pre = (selected * grad_act).astype(jnp.bfloat16)
    grad_part = lax.dot_general(
        grad_pre, encoder[0], (((1,), (1,)), ((), ())), preferred_element_type=jnp.float32
    )
    grad_blocks = (
        grad_part.reshape(2, half_rows, feat_parts, cols)
        .transpose(0, 2, 1, 3)
        .reshape(2 * feat_parts, half_rows, cols)
    )
    grad_sum = reduce_scatter(grad_blocks, PLANE)
    return (error, grad_sum.astype(jnp.bfloat16)[None])


def solution(mesh):
    layer_n = mesh.shape["layer"]
    feat_n = mesh.shape["feat"]
    split = Mesh(mesh.devices.reshape(layer_n // 2, 2, feat_n), ("lz", "lx", "feat"))
    slot = ("lz", "lx")
    in_specs = (
        P(slot, None, "feat"),
        P(slot, None, "feat"),
        P(slot, "feat"),
        P(slot, None, "feat", None),
        P(None, "feat"),
        P(),
        P(None, slot, "feat"),
    )
    out_specs = (P(None, slot, "feat"), P(slot, None, "feat"))
    return jax.shard_map(local, mesh=split, in_specs=in_specs, out_specs=out_specs, check_vma=False)
```

```python
import jax
import jax.numpy as jnp
from jax import lax
from jax.sharding import Mesh
from jax.sharding import PartitionSpec as P

PLANE = ("lx", "feat")
EVERY = ("lz", "lx", "feat")


def bit_labels(axes):
    labels = []
    for axis in axes:
        size = lax.axis_size(axis)
        bits = size.bit_length() - 1
        assert 1 << bits == size
        labels += [(axis, b) for b in reversed(range(bits))]
    return labels


def plan(axes):
    labels = bit_labels(axes)
    prefix = [("feat", 0)]
    suffix = [("lz", lax.axis_size("lz").bit_length() - 2)] if "lz" in axes else []
    rotation = [label for label in labels if label not in prefix + suffix]
    orders = [rotation[p:] + rotation[:p] for p in range(len(rotation))]
    return labels, prefix, orders, suffix


def row_split(rows, parts):
    base = (rows // (8 * parts)) * 8
    sizes = [base] * parts
    extra = rows - base * parts
    i = 0
    while extra >= 8:
        sizes[i % parts] += 8
        extra -= 8
        i += 1
    sizes[0] += extra
    return sizes


def partner(axis, bit):
    return [(i, i ^ (1 << bit)) for i in range(lax.axis_size(axis))]


def portion_rows(rows, parts):
    sizes = row_split(rows, parts)
    return [(sum(sizes[:i]), sizes[i]) for i in range(parts)]


def reduce_scatter(blocks, axes):
    labels, prefix, orders, suffix = plan(axes)
    n, rows, cols = blocks.shape
    nb = len(labels)
    x = blocks.reshape([2] * nb + [rows, cols])
    steps = [prefix + order + suffix for order in orders]
    parts = []
    for (start, size), order in zip(portion_rows(rows, len(orders)), steps):
        xp = lax.slice_in_dim(x, start, start + size, axis=nb)
        xp = jnp.transpose(xp, [labels.index(l) for l in order] + [nb, nb + 1])
        parts.append(xp.reshape(n, size, cols))
    for k in range(nb):
        for p in range(len(parts)):
            axis, bit = steps[p][k]
            own = (lax.axis_index(axis) >> bit) & 1
            half = parts[p].shape[0] // 2
            keep = lax.dynamic_slice_in_dim(parts[p], own * half, half, 0)
            send = lax.dynamic_slice_in_dim(parts[p], (1 - own) * half, half, 0)
            parts[p] = keep + lax.ppermute(send, axis, partner(axis, bit))
    return jnp.concatenate([xp[0] for xp in parts], axis=0)


def all_gather(block, axes):
    labels, prefix, orders, suffix = plan(axes)
    rows, cols = block.shape
    nb = len(labels)
    steps = [prefix + order + suffix for order in orders]
    spans = portion_rows(rows, len(orders))
    parts = [lax.slice_in_dim(block, start, start + size, axis=0)[None] for start, size in spans]
    for k in reversed(range(nb)):
        for p in range(len(parts)):
            axis, bit = steps[p][k]
            own = (lax.axis_index(axis) >> bit) & 1
            recv = lax.ppermute(parts[p], axis, partner(axis, bit))
            parts[p] = jnp.where(
                own == 0, jnp.concatenate([parts[p], recv]), jnp.concatenate([recv, parts[p]])
            )
    out = []
    for xp, order, (start, size) in zip(parts, steps, spans):
        xp = xp.reshape([2] * nb + [size, cols])
        xp = jnp.transpose(xp, [order.index(l) for l in labels] + [nb, nb + 1])
        out.append(xp.reshape(-1, size, cols))
    return jnp.concatenate(out, axis=1)


def local(resid, encoder, encoder_bias, decoder, decoder_bias, topk_index, target):
    planes = lax.axis_size("lz")
    feat_parts = lax.axis_size("feat")
    layer_id = lax.axis_index("lz")
    half_bit = lax.axis_index("lx")
    feat_pos = lax.axis_index("feat")
    layer_count = decoder.shape[1]
    feat_dev = encoder.shape[2]
    half_rows = resid.shape[1]
    cols = resid.shape[2]
    tokens = 2 * half_rows
    width = cols * feat_parts
    slots = 2 * planes
    slot_rows = tokens // slots
    feat_total = 2 * feat_parts * feat_dev

    gathered = all_gather(resid[0], PLANE)
    tokens_all = (
        gathered.reshape(2, feat_parts, half_rows, cols).transpose(0, 2, 1, 3).reshape(tokens, width)
    )
    pre = jnp.dot(tokens_all, encoder[0], preferred_element_type=jnp.float32) + encoder_bias[0]
    first_feat = half_bit * (feat_total // 2) + feat_pos * feat_dev
    feat_ids = first_feat + lax.iota(jnp.int32, feat_dev)
    layer_index = lax.dynamic_index_in_dim(topk_index, layer_id, 0, keepdims=False)
    selected = jnp.any(layer_index[:, :, None] == feat_ids[None, None, :], axis=1).astype(
        jnp.float32
    )
    acts = (selected * pre).astype(jnp.bfloat16)
    live_layers = lax.iota(jnp.int32, layer_count) >= layer_id
    partial_value = jnp.einsum("tf,lfd->ltd", acts, decoder[0], preferred_element_type=jnp.float32)
    partial_value = jnp.where(live_layers[:, None, None], partial_value, 0.0)
    blocks = (
        partial_value.reshape(layer_count, slots, slot_rows, feat_parts, cols)
        .transpose(1, 3, 0, 2, 4)
        .reshape(slots * feat_parts, layer_count * slot_rows, cols)
    )
    recon = reduce_scatter(blocks, EVERY).reshape(layer_count, slot_rows, cols)
    recon = recon + decoder_bias[:, None, :]
    error = (recon - target.astype(jnp.float32)).astype(jnp.bfloat16)
    pieces = all_gather(error.reshape(layer_count * slot_rows, cols), EVERY)
    piece = (
        pieces.reshape(slots, feat_parts, layer_count, slot_rows, cols)
        .transpose(2, 0, 3, 1, 4)
        .reshape(layer_count, tokens, width)
    )
    kept = jnp.where(live_layers[:, None, None], piece, jnp.zeros_like(piece))
    grad_act = jnp.einsum("ltd,lfd->tf", kept, decoder[0], preferred_element_type=jnp.float32)
    grad_pre = (selected * grad_act).astype(jnp.bfloat16)
    grad_part = lax.dot_general(
        grad_pre, encoder[0], (((1,), (1,)), ((), ())), preferred_element_type=jnp.float32
    )
    grad_blocks = (
        grad_part.reshape(2, half_rows, feat_parts, cols)
        .transpose(0, 2, 1, 3)
        .reshape(2 * feat_parts, half_rows, cols)
    )
    grad_sum = reduce_scatter(grad_blocks, PLANE)
    return (error, grad_sum.astype(jnp.bfloat16)[None])


def solution(mesh):
    layer_n = mesh.shape["layer"]
    feat_n = mesh.shape["feat"]
    split = Mesh(mesh.devices.reshape(layer_n // 2, 2, feat_n), ("lz", "lx", "feat"))
    slot = ("lz", "lx")
    in_specs = (
        P(slot, None, "feat"),
        P(slot, None, "feat"),
        P(slot, "feat"),
        P(slot, None, "feat", None),
        P(None, "feat"),
        P(),
        P(None, slot, "feat"),
    )
    out_specs = (P(None, slot, "feat"), P(slot, None, "feat"))
    return jax.shard_map(local, mesh=split, in_specs=in_specs, out_specs=out_specs, check_vma=False)
```

```python
import jax
import jax.numpy as jnp
from jax import lax
from jax.sharding import Mesh
from jax.sharding import PartitionSpec as P

PLANE = ("lx", "feat")
EVERY = ("lz", "lx", "feat")


def bit_labels(axes):
    labels = []
    for axis in axes:
        size = lax.axis_size(axis)
        bits = size.bit_length() - 1
        assert 1 << bits == size
        labels += [(axis, b) for b in reversed(range(bits))]
    return labels


def plan(axes):
    labels = bit_labels(axes)
    prefix = [("feat", 0)]
    suffix = [("lz", lax.axis_size("lz").bit_length() - 2)] if "lz" in axes else []
    rotation = [label for label in labels if label not in prefix + suffix]
    orders = [rotation[p:] + rotation[:p] for p in range(len(rotation))]
    return labels, prefix, orders, suffix


def row_split(rows, parts):
    base = (rows // (8 * parts)) * 8
    sizes = [base] * parts
    extra = rows - base * parts
    i = 0
    while extra >= 8:
        sizes[i % parts] += 8
        extra -= 8
        i += 1
    sizes[0] += extra
    return sizes


def partner(axis, bit):
    return [(i, i ^ (1 << bit)) for i in range(lax.axis_size(axis))]


def portion_rows(rows, parts):
    sizes = row_split(rows, parts)
    return [(sum(sizes[:i]), sizes[i]) for i in range(parts)]


def reduce_scatter(blocks, axes, wire):
    labels, prefix, orders, suffix = plan(axes)
    n, rows, cols = blocks.shape
    nb = len(labels)
    x = blocks.reshape([2] * nb + [rows, cols])
    steps = [prefix + order + suffix for order in orders]
    parts = []
    for (start, size), order in zip(portion_rows(rows, len(orders)), steps):
        xp = lax.slice_in_dim(x, start, start + size, axis=nb)
        xp = jnp.transpose(xp, [labels.index(l) for l in order] + [nb, nb + 1])
        parts.append(xp.reshape(n, size, cols))
    for k in range(nb):
        for p in range(len(parts)):
            axis, bit = steps[p][k]
            own = (lax.axis_index(axis) >> bit) & 1
            half = parts[p].shape[0] // 2
            keep = lax.dynamic_slice_in_dim(parts[p], own * half, half, 0)
            send = lax.dynamic_slice_in_dim(parts[p], (1 - own) * half, half, 0)
            recv = lax.ppermute(send.astype(wire), axis, partner(axis, bit))
            parts[p] = keep + recv.astype(keep.dtype)
    return jnp.concatenate([xp[0] for xp in parts], axis=0)


def all_gather(block, axes):
    labels, prefix, orders, suffix = plan(axes)
    rows, cols = block.shape
    nb = len(labels)
    steps = [prefix + order + suffix for order in orders]
    spans = portion_rows(rows, len(orders))
    parts = [lax.slice_in_dim(block, start, start + size, axis=0)[None] for start, size in spans]
    for k in reversed(range(nb)):
        for p in range(len(parts)):
            axis, bit = steps[p][k]
            own = (lax.axis_index(axis) >> bit) & 1
            recv = lax.ppermute(parts[p], axis, partner(axis, bit))
            parts[p] = jnp.where(
                own == 0, jnp.concatenate([parts[p], recv]), jnp.concatenate([recv, parts[p]])
            )
    out = []
    for xp, order, (start, size) in zip(parts, steps, spans):
        xp = xp.reshape([2] * nb + [size, cols])
        xp = jnp.transpose(xp, [order.index(l) for l in labels] + [nb, nb + 1])
        out.append(xp.reshape(-1, size, cols))
    return jnp.concatenate(out, axis=1)


def local(resid, encoder, encoder_bias, decoder, decoder_bias, topk_index, target):
    planes = lax.axis_size("lz")
    feat_parts = lax.axis_size("feat")
    layer_id = lax.axis_index("lz")
    half_bit = lax.axis_index("lx")
    feat_pos = lax.axis_index("feat")
    layer_count = decoder.shape[1]
    feat_dev = encoder.shape[2]
    half_rows = resid.shape[1]
    cols = resid.shape[2]
    tokens = 2 * half_rows
    width = cols * feat_parts
    slots = 2 * planes
    slot_rows = tokens // slots
    feat_total = 2 * feat_parts * feat_dev

    gathered = all_gather(resid[0], PLANE)
    tokens_all = (
        gathered.reshape(2, feat_parts, half_rows, cols).transpose(0, 2, 1, 3).reshape(tokens, width)
    )
    pre = jnp.dot(tokens_all, encoder[0], preferred_element_type=jnp.float32) + encoder_bias[0]
    first_feat = half_bit * (feat_total // 2) + feat_pos * feat_dev
    feat_ids = first_feat + lax.iota(jnp.int32, feat_dev)
    layer_index = lax.dynamic_index_in_dim(topk_index, layer_id, 0, keepdims=False)
    selected = jnp.any(layer_index[:, :, None] == feat_ids[None, None, :], axis=1).astype(
        jnp.float32
    )
    acts = (selected * pre).astype(jnp.bfloat16)
    live_layers = lax.iota(jnp.int32, layer_count) >= layer_id
    partial_value = jnp.einsum("tf,lfd->ltd", acts, decoder[0], preferred_element_type=jnp.float32)
    partial_value = jnp.where(live_layers[:, None, None], partial_value, 0.0)
    blocks = (
        partial_value.reshape(layer_count, slots, slot_rows, feat_parts, cols)
        .transpose(1, 3, 0, 2, 4)
        .reshape(slots * feat_parts, layer_count * slot_rows, cols)
    )
    recon = reduce_scatter(blocks, EVERY, jnp.bfloat16).reshape(layer_count, slot_rows, cols)
    recon = recon + decoder_bias[:, None, :]
    error = (recon - target.astype(jnp.float32)).astype(jnp.bfloat16)
    pieces = all_gather(error.reshape(layer_count * slot_rows, cols), EVERY)
    piece = (
        pieces.reshape(slots, feat_parts, layer_count, slot_rows, cols)
        .transpose(2, 0, 3, 1, 4)
        .reshape(layer_count, tokens, width)
    )
    kept = jnp.where(live_layers[:, None, None], piece, jnp.zeros_like(piece))
    grad_act = jnp.einsum("ltd,lfd->tf", kept, decoder[0], preferred_element_type=jnp.float32)
    grad_pre = (selected * grad_act).astype(jnp.bfloat16)
    grad_part = lax.dot_general(
        grad_pre, encoder[0], (((1,), (1,)), ((), ())), preferred_element_type=jnp.float32
    )
    grad_blocks = (
        grad_part.reshape(2, half_rows, feat_parts, cols)
        .transpose(0, 2, 1, 3)
        .reshape(2 * feat_parts, half_rows, cols)
    )
    grad_sum = reduce_scatter(grad_blocks, PLANE, jnp.bfloat16)
    return (error, grad_sum.astype(jnp.bfloat16)[None])


def solution(mesh):
    layer_n = mesh.shape["layer"]
    feat_n = mesh.shape["feat"]
    split = Mesh(mesh.devices.reshape(layer_n // 2, 2, feat_n), ("lz", "lx", "feat"))
    slot = ("lz", "lx")
    in_specs = (
        P(slot, None, "feat"),
        P(slot, None, "feat"),
        P(slot, "feat"),
        P(slot, None, "feat", None),
        P(None, "feat"),
        P(),
        P(None, slot, "feat"),
    )
    out_specs = (P(None, slot, "feat"), P(slot, None, "feat"))
    return jax.shard_map(local, mesh=split, in_specs=in_specs, out_specs=out_specs, check_vma=False)
```

```python
import jax
import jax.numpy as jnp
from jax import lax
from jax.sharding import Mesh
from jax.sharding import PartitionSpec as P

PLANE = ("lx", "feat")
EVERY = ("lz", "lx", "feat")


def bit_labels(axes):
    labels = []
    for axis in axes:
        size = lax.axis_size(axis)
        bits = size.bit_length() - 1
        assert 1 << bits == size
        labels += [(axis, b) for b in reversed(range(bits))]
    return labels


def plan(axes):
    labels = bit_labels(axes)
    prefix = [("feat", 0)]
    suffix = [("lz", lax.axis_size("lz").bit_length() - 2)] if "lz" in axes else []
    rotation = [label for label in labels if label not in prefix + suffix]
    orders = [rotation[p:] + rotation[:p] for p in range(len(rotation))]
    return labels, prefix, orders, suffix


def row_split(rows, parts):
    base = (rows // (8 * parts)) * 8
    sizes = [base] * parts
    extra = rows - base * parts
    i = 0
    while extra >= 8:
        sizes[i % parts] += 8
        extra -= 8
        i += 1
    sizes[0] += extra
    return sizes


def partner(axis, bit):
    return [(i, i ^ (1 << bit)) for i in range(lax.axis_size(axis))]


def portion_rows(rows, parts):
    sizes = row_split(rows, parts)
    return [(sum(sizes[:i]), sizes[i]) for i in range(parts)]


def reduce_scatter(blocks, axes, wire):
    labels, prefix, orders, suffix = plan(axes)
    n, rows, cols = blocks.shape
    nb = len(labels)
    x = blocks.reshape([2] * nb + [rows, cols])
    steps = [prefix + order + suffix for order in orders]
    parts = []
    for (start, size), order in zip(portion_rows(rows, len(orders)), steps):
        xp = lax.slice_in_dim(x, start, start + size, axis=nb)
        xp = jnp.transpose(xp, [labels.index(l) for l in order] + [nb, nb + 1])
        parts.append(xp.reshape(n, size, cols))
    for k in range(nb):
        for p in range(len(parts)):
            axis, bit = steps[p][k]
            own = (lax.axis_index(axis) >> bit) & 1
            half = parts[p].shape[0] // 2
            keep = lax.dynamic_slice_in_dim(parts[p], own * half, half, 0)
            send = lax.dynamic_slice_in_dim(parts[p], (1 - own) * half, half, 0)
            recv = lax.ppermute(send.astype(wire), axis, partner(axis, bit))
            parts[p] = keep + recv.astype(keep.dtype)
    return jnp.concatenate([xp[0] for xp in parts], axis=0)


def all_gather(block, axes):
    labels, prefix, orders, suffix = plan(axes)
    rows, cols = block.shape
    nb = len(labels)
    steps = [prefix + order + suffix for order in orders]
    spans = portion_rows(rows, len(orders))
    parts = [lax.slice_in_dim(block, start, start + size, axis=0)[None] for start, size in spans]
    for k in reversed(range(nb)):
        for p in range(len(parts)):
            axis, bit = steps[p][k]
            own = (lax.axis_index(axis) >> bit) & 1
            recv = lax.ppermute(parts[p], axis, partner(axis, bit))
            parts[p] = jnp.where(
                own == 0, jnp.concatenate([parts[p], recv]), jnp.concatenate([recv, parts[p]])
            )
    out = []
    for xp, order, (start, size) in zip(parts, steps, spans):
        xp = xp.reshape([2] * nb + [size, cols])
        xp = jnp.transpose(xp, [order.index(l) for l in labels] + [nb, nb + 1])
        out.append(xp.reshape(-1, size, cols))
    return jnp.concatenate(out, axis=1)


def local(resid, encoder, encoder_bias, decoder, decoder_bias, topk_index, target):
    planes = lax.axis_size("lz")
    feat_parts = lax.axis_size("feat")
    layer_id = lax.axis_index("lz")
    half_bit = lax.axis_index("lx")
    feat_pos = lax.axis_index("feat")
    layer_count = decoder.shape[1]
    feat_dev = encoder.shape[2]
    half_rows = resid.shape[1]
    cols = resid.shape[2]
    tokens = 2 * half_rows
    width = cols * feat_parts
    slots = 2 * planes
    slot_rows = tokens // slots
    feat_total = 2 * feat_parts * feat_dev

    enc_chunks = encoder[0].reshape(feat_parts, cols, feat_dev)
    dec_chunks = decoder[0].reshape(layer_count, feat_dev, feat_parts, cols).transpose(2, 0, 1, 3)

    gathered = all_gather(resid[0], PLANE)
    tokens_chunks = (
        gathered.reshape(2, feat_parts, half_rows, cols).transpose(1, 0, 2, 3).reshape(feat_parts, tokens, cols)
    )
    pre = jnp.einsum("cte,cef->tf", tokens_chunks, enc_chunks, preferred_element_type=jnp.float32)
    pre = pre + encoder_bias[0]
    first_feat = half_bit * (feat_total // 2) + feat_pos * feat_dev
    feat_ids = first_feat + lax.iota(jnp.int32, feat_dev)
    layer_index = lax.dynamic_index_in_dim(topk_index, layer_id, 0, keepdims=False)
    selected = jnp.any(layer_index[:, :, None] == feat_ids[None, None, :], axis=1).astype(
        jnp.float32
    )
    acts = (selected * pre).astype(jnp.bfloat16)
    live_layers = lax.iota(jnp.int32, layer_count) >= layer_id
    partial_value = jnp.einsum("tf,clfe->clte", acts, dec_chunks, preferred_element_type=jnp.float32)
    partial_value = jnp.where(live_layers[None, :, None, None], partial_value, 0.0)
    blocks = (
        partial_value.reshape(feat_parts, layer_count, slots, slot_rows, cols)
        .transpose(2, 0, 1, 3, 4)
        .reshape(slots * feat_parts, layer_count * slot_rows, cols)
    )
    recon = reduce_scatter(blocks, EVERY, jnp.bfloat16).reshape(layer_count, slot_rows, cols)
    recon = recon + decoder_bias[:, None, :]
    error = (recon - target.astype(jnp.float32)).astype(jnp.bfloat16)
    pieces = all_gather(error.reshape(layer_count * slot_rows, cols), EVERY)
    piece = (
        pieces.reshape(slots, feat_parts, layer_count, slot_rows, cols)
        .transpose(1, 2, 0, 3, 4)
        .reshape(feat_parts, layer_count, tokens, cols)
    )
    kept = jnp.where(live_layers[None, :, None, None], piece, jnp.zeros_like(piece))
    grad_act = jnp.einsum("clte,clfe->tf", kept, dec_chunks, preferred_element_type=jnp.float32)
    grad_pre = (selected * grad_act).astype(jnp.bfloat16)
    grad_part = jnp.einsum("tf,cef->cte", grad_pre, enc_chunks, preferred_element_type=jnp.float32)
    grad_blocks = (
        grad_part.reshape(feat_parts, 2, half_rows, cols)
        .transpose(1, 0, 2, 3)
        .reshape(2 * feat_parts, half_rows, cols)
    )
    grad_sum = reduce_scatter(grad_blocks, PLANE, jnp.bfloat16)
    return (error, grad_sum.astype(jnp.bfloat16)[None])


def solution(mesh):
    layer_n = mesh.shape["layer"]
    feat_n = mesh.shape["feat"]
    split = Mesh(mesh.devices.reshape(layer_n // 2, 2, feat_n), ("lz", "lx", "feat"))
    slot = ("lz", "lx")
    in_specs = (
        P(slot, None, "feat"),
        P(slot, None, "feat"),
        P(slot, "feat"),
        P(slot, None, "feat", None),
        P(None, "feat"),
        P(),
        P(None, slot, "feat"),
    )
    out_specs = (P(None, slot, "feat"), P(slot, None, "feat"))
    return jax.shard_map(local, mesh=split, in_specs=in_specs, out_specs=out_specs, check_vma=False)
```

```python
import jax
import jax.numpy as jnp
from jax import lax
from jax.sharding import Mesh
from jax.sharding import PartitionSpec as P

PLANE = ("lx", "feat")
EVERY = ("lz", "lx", "feat")


def bit_labels(axes):
    labels = []
    for axis in axes:
        size = lax.axis_size(axis)
        bits = size.bit_length() - 1
        assert 1 << bits == size
        labels += [(axis, b) for b in reversed(range(bits))]
    return labels


def plan(axes):
    labels = bit_labels(axes)
    prefix = [("feat", 0)]
    suffix = [("lz", lax.axis_size("lz").bit_length() - 2)] if "lz" in axes else []
    rotation = [label for label in labels if label not in prefix + suffix]
    orders = [rotation[p:] + rotation[:p] for p in range(len(rotation))]
    return labels, prefix, orders, suffix


def row_split(rows, parts):
    base = (rows // (8 * parts)) * 8
    sizes = [base] * parts
    extra = rows - base * parts
    i = 0
    while extra >= 8:
        sizes[i % parts] += 8
        extra -= 8
        i += 1
    sizes[0] += extra
    return sizes


def partner(axis, bit):
    return [(i, i ^ (1 << bit)) for i in range(lax.axis_size(axis))]


def portion_rows(rows, parts):
    sizes = row_split(rows, parts)
    return [(sum(sizes[:i]), sizes[i]) for i in range(parts)]


def reduce_scatter(blocks, axes, wire):
    labels, prefix, orders, suffix = plan(axes)
    nb = len(labels)
    steps = [prefix + order + suffix for order in orders]
    parts = []
    for (start, size), order in zip(portion_rows(blocks.rows, len(orders)), steps):
        parts.append(blocks.portion([labels.index(l) for l in order], start, size))
    for k in range(nb):
        for p in range(len(parts)):
            axis, bit = steps[p][k]
            own = (lax.axis_index(axis) >> bit) & 1
            half = parts[p].shape[0] // 2
            keep = lax.dynamic_slice_in_dim(parts[p], own * half, half, 0)
            send = lax.dynamic_slice_in_dim(parts[p], (1 - own) * half, half, 0)
            recv = lax.ppermute(send.astype(wire), axis, partner(axis, bit))
            parts[p] = keep + recv.astype(keep.dtype)
    return jnp.concatenate([xp[0] for xp in parts], axis=0)


def all_gather(block, axes):
    labels, prefix, orders, suffix = plan(axes)
    rows, cols = block.shape
    nb = len(labels)
    steps = [prefix + order + suffix for order in orders]
    spans = portion_rows(rows, len(orders))
    parts = [lax.slice_in_dim(block, start, start + size, axis=0)[None] for start, size in spans]
    for k in reversed(range(nb)):
        for p in range(len(parts)):
            axis, bit = steps[p][k]
            own = (lax.axis_index(axis) >> bit) & 1
            recv = lax.ppermute(parts[p], axis, partner(axis, bit))
            parts[p] = jnp.where(
                own == 0, jnp.concatenate([parts[p], recv]), jnp.concatenate([recv, parts[p]])
            )
    out = []
    for xp, order, (start, size) in zip(parts, steps, spans):
        xp = xp.reshape([2] * nb + [size, cols])
        xp = jnp.transpose(xp, [order.index(l) for l in labels] + [nb, nb + 1])
        out.append(xp.reshape(-1, size, cols))
    return jnp.concatenate(out, axis=1)


class Blocks:
    def __init__(self, array, bit_axes, row_axes, cols):
        self.array, self.bit_axes, self.row_axes, self.cols = array, bit_axes, row_axes, cols
        self.rows = 1
        for axis in row_axes:
            self.rows *= array.shape[axis]

    def portion(self, bit_order, start, size):
        (row_axis,) = self.row_axes
        x = lax.slice_in_dim(self.array, start, start + size, axis=row_axis)
        order = [self.bit_axes[b] for b in bit_order] + [row_axis, self.array.ndim - 1]
        return jnp.transpose(x, order).reshape(2 ** len(bit_order), size, self.cols)


def local(resid, encoder, encoder_bias, decoder, decoder_bias, topk_index, target):
    planes = lax.axis_size("lz")
    feat_parts = lax.axis_size("feat")
    layer_id = lax.axis_index("lz")
    half_bit = lax.axis_index("lx")
    feat_pos = lax.axis_index("feat")
    layer_count = decoder.shape[1]
    feat_dev = encoder.shape[2]
    half_rows = resid.shape[1]
    cols = resid.shape[2]
    tokens = 2 * half_rows
    width = cols * feat_parts
    slots = 2 * planes
    slot_rows = tokens // slots
    feat_total = 2 * feat_parts * feat_dev

    gathered = all_gather(resid[0], PLANE)
    tokens_all = (
        gathered.reshape(2, feat_parts, half_rows, cols).transpose(0, 2, 1, 3).reshape(tokens, width)
    )
    pre = jnp.dot(tokens_all, encoder[0], preferred_element_type=jnp.float32) + encoder_bias[0]
    first_feat = half_bit * (feat_total // 2) + feat_pos * feat_dev
    feat_ids = first_feat + lax.iota(jnp.int32, feat_dev)
    layer_index = lax.dynamic_index_in_dim(topk_index, layer_id, 0, keepdims=False)
    selected = jnp.any(layer_index.T[:, :, None] == feat_ids[None, None, :], axis=0).astype(
        jnp.float32
    )
    acts = (selected * pre).astype(jnp.bfloat16)
    live_layers = lax.iota(jnp.int32, layer_count) >= layer_id
    partial_value = jnp.einsum("tf,lfd->ltd", acts, decoder[0], preferred_element_type=jnp.float32)
    partial_value = jnp.where(live_layers[:, None, None], partial_value, 0.0)
    slot_bits = slots.bit_length() - 1
    feat_bits = feat_parts.bit_length() - 1
    every_bits = slot_bits + feat_bits
    ordered = (
        partial_value.reshape(layer_count, slots, slot_rows, feat_parts, cols)
        .transpose(1, 3, 0, 2, 4)
        .reshape([2] * every_bits + [layer_count * slot_rows, cols])
    )
    blocks = Blocks(ordered, list(range(every_bits)), (every_bits,), cols)
    recon = reduce_scatter(blocks, EVERY, jnp.bfloat16).reshape(layer_count, slot_rows, cols)
    recon = recon + decoder_bias[:, None, :]
    error = (recon - target.astype(jnp.float32)).astype(jnp.bfloat16)
    pieces = all_gather(error.reshape(layer_count * slot_rows, cols), EVERY)
    piece = (
        pieces.reshape(slots, feat_parts, layer_count, slot_rows, cols)
        .transpose(2, 0, 3, 1, 4)
        .reshape(layer_count, tokens, width)
    )
    kept = jnp.where(live_layers[:, None, None], piece, jnp.zeros_like(piece))
    grad_act = jnp.einsum("ltd,lfd->tf", kept, decoder[0], preferred_element_type=jnp.float32)
    grad_pre = (selected * grad_act).astype(jnp.bfloat16)
    enc_chunks = encoder[0].reshape(feat_parts, cols, feat_dev)
    grad_part = jnp.einsum("tf,cef->cte", grad_pre, enc_chunks, preferred_element_type=jnp.float32)
    grad_shaped = grad_part.reshape([2] * feat_bits + [2, half_rows, cols])
    grad_blocks = Blocks(grad_shaped, [feat_bits] + list(range(feat_bits)), (feat_bits + 1,), cols)
    grad_sum = reduce_scatter(grad_blocks, PLANE, jnp.bfloat16)
    return (error, grad_sum.astype(jnp.bfloat16)[None])


def solution(mesh):
    layer_n = mesh.shape["layer"]
    feat_n = mesh.shape["feat"]
    split = Mesh(mesh.devices.reshape(layer_n // 2, 2, feat_n), ("lz", "lx", "feat"))
    slot = ("lz", "lx")
    in_specs = (
        P(slot, None, "feat"),
        P(slot, None, "feat"),
        P(slot, "feat"),
        P(slot, None, "feat", None),
        P(None, "feat"),
        P(),
        P(None, slot, "feat"),
    )
    out_specs = (P(None, slot, "feat"), P(slot, None, "feat"))
    return jax.shard_map(local, mesh=split, in_specs=in_specs, out_specs=out_specs, check_vma=False)
```

```python
import jax
import jax.numpy as jnp
from jax import lax
from jax.sharding import Mesh
from jax.sharding import PartitionSpec as P

PLANE = ("lx", "feat")
EVERY = ("lz", "lx", "feat")


def bit_labels(axes):
    labels = []
    for axis in axes:
        size = lax.axis_size(axis)
        bits = size.bit_length() - 1
        assert 1 << bits == size
        labels += [(axis, b) for b in reversed(range(bits))]
    return labels


def plan(axes):
    labels = bit_labels(axes)
    prefix = [("feat", 0)]
    suffix = [("lz", lax.axis_size("lz").bit_length() - 2)] if "lz" in axes else []
    rotation = [label for label in labels if label not in prefix + suffix]
    orders = [rotation[p:] + rotation[:p] for p in range(len(rotation))]
    return labels, prefix, orders, suffix


def row_split(rows, parts):
    base = (rows // (8 * parts)) * 8
    sizes = [base] * parts
    extra = rows - base * parts
    i = 0
    while extra >= 8:
        sizes[i % parts] += 8
        extra -= 8
        i += 1
    sizes[0] += extra
    return sizes


def partner(axis, bit):
    return [(i, i ^ (1 << bit)) for i in range(lax.axis_size(axis))]


def portion_rows(rows, parts):
    sizes = row_split(rows, parts)
    return [(sum(sizes[:i]), sizes[i]) for i in range(parts)]


def reduce_scatter(blocks, axes, wire):
    labels, prefix, orders, suffix = plan(axes)
    n, rows, cols = blocks.shape
    nb = len(labels)
    x = blocks.reshape([2] * nb + [rows, cols])
    steps = [prefix + order + suffix for order in orders]
    parts = []
    for (start, size), order in zip(portion_rows(rows, len(orders)), steps):
        xp = lax.slice_in_dim(x, start, start + size, axis=nb)
        xp = jnp.transpose(xp, [labels.index(l) for l in order] + [nb, nb + 1])
        parts.append(xp.reshape(n, size, cols))
    for k in range(nb):
        for p in range(len(parts)):
            axis, bit = steps[p][k]
            own = (lax.axis_index(axis) >> bit) & 1
            half = parts[p].shape[0] // 2
            keep = lax.dynamic_slice_in_dim(parts[p], own * half, half, 0)
            send = lax.dynamic_slice_in_dim(parts[p], (1 - own) * half, half, 0)
            recv = lax.ppermute(send.astype(wire), axis, partner(axis, bit))
            parts[p] = keep + recv.astype(keep.dtype)
    return jnp.concatenate([xp[0] for xp in parts], axis=0)


def all_gather(block, axes):
    labels, prefix, orders, suffix = plan(axes)
    rows, cols = block.shape
    nb = len(labels)
    steps = [prefix + order + suffix for order in orders]
    spans = portion_rows(rows, len(orders))
    parts = [lax.slice_in_dim(block, start, start + size, axis=0)[None] for start, size in spans]
    for k in reversed(range(nb)):
        for p in range(len(parts)):
            axis, bit = steps[p][k]
            own = (lax.axis_index(axis) >> bit) & 1
            recv = lax.ppermute(parts[p], axis, partner(axis, bit))
            parts[p] = jnp.where(
                own == 0, jnp.concatenate([parts[p], recv]), jnp.concatenate([recv, parts[p]])
            )
    out = []
    for xp, order, (start, size) in zip(parts, steps, spans):
        xp = xp.reshape([2] * nb + [size, cols])
        xp = jnp.transpose(xp, [order.index(l) for l in labels] + [nb, nb + 1])
        out.append(xp.reshape(-1, size, cols))
    return jnp.concatenate(out, axis=1)


def local(resid, encoder, encoder_bias, decoder, decoder_bias, topk_index, target):
    planes = lax.axis_size("lz")
    feat_parts = lax.axis_size("feat")
    layer_id = lax.axis_index("lz")
    half_bit = lax.axis_index("lx")
    feat_pos = lax.axis_index("feat")
    layer_count = decoder.shape[1]
    feat_dev = encoder.shape[2]
    half_rows = resid.shape[1]
    cols = resid.shape[2]
    tokens = 2 * half_rows
    width = cols * feat_parts
    slots = 2 * planes
    slot_rows = tokens // slots
    feat_total = 2 * feat_parts * feat_dev

    gathered = all_gather(resid[0], PLANE)
    tokens_all = (
        gathered.reshape(2, feat_parts, half_rows, cols).transpose(0, 2, 1, 3).reshape(tokens, width)
    )
    pre = jnp.dot(tokens_all, encoder[0], preferred_element_type=jnp.float32) + encoder_bias[0]
    first_feat = half_bit * (feat_total // 2) + feat_pos * feat_dev
    feat_ids = first_feat + lax.iota(jnp.int32, feat_dev)
    layer_index = lax.dynamic_index_in_dim(topk_index, layer_id, 0, keepdims=False)
    selected = jnp.any(layer_index[:, :, None] == feat_ids[None, None, :], axis=1).astype(
        jnp.float32
    )
    acts = (selected * pre).astype(jnp.bfloat16)
    live_layers = lax.iota(jnp.int32, layer_count) >= layer_id
    groups = 2 if layer_count % 2 == 0 else 1
    per_group = layer_count // groups
    errors = []
    for g in range(groups):
        chosen = slice(g * per_group, (g + 1) * per_group)
        live = live_layers[chosen]
        partial_value = jnp.einsum(
            "tf,lfd->ltd", acts, decoder[0, chosen], preferred_element_type=jnp.float32
        )
        partial_value = jnp.where(live[:, None, None], partial_value, 0.0)
        blocks = (
            partial_value.reshape(per_group, slots, slot_rows, feat_parts, cols)
            .transpose(1, 3, 0, 2, 4)
            .reshape(slots * feat_parts, per_group * slot_rows, cols)
        )
        recon = reduce_scatter(blocks, EVERY, jnp.bfloat16).reshape(per_group, slot_rows, cols)
        recon = recon + decoder_bias[chosen, None, :]
        errors.append((recon - target[chosen].astype(jnp.float32)).astype(jnp.bfloat16))
    grad_act = None
    for g in range(groups):
        chosen = slice(g * per_group, (g + 1) * per_group)
        live = live_layers[chosen]
        pieces = all_gather(errors[g].reshape(per_group * slot_rows, cols), EVERY)
        piece = (
            pieces.reshape(slots, feat_parts, per_group, slot_rows, cols)
            .transpose(2, 0, 3, 1, 4)
            .reshape(per_group, tokens, width)
        )
        kept = jnp.where(live[:, None, None], piece, jnp.zeros_like(piece))
        term = jnp.einsum("ltd,lfd->tf", kept, decoder[0, chosen], preferred_element_type=jnp.float32)
        grad_act = term if grad_act is None else grad_act + term
    error = jnp.concatenate(errors, axis=0)
    grad_pre = (selected * grad_act).astype(jnp.bfloat16)
    grad_part = lax.dot_general(
        grad_pre, encoder[0], (((1,), (1,)), ((), ())), preferred_element_type=jnp.float32
    )
    grad_blocks = (
        grad_part.reshape(2, half_rows, feat_parts, cols)
        .transpose(0, 2, 1, 3)
        .reshape(2 * feat_parts, half_rows, cols)
    )
    grad_sum = reduce_scatter(grad_blocks, PLANE, jnp.bfloat16)
    return (error, grad_sum.astype(jnp.bfloat16)[None])


def solution(mesh):
    layer_n = mesh.shape["layer"]
    feat_n = mesh.shape["feat"]
    split = Mesh(mesh.devices.reshape(layer_n // 2, 2, feat_n), ("lz", "lx", "feat"))
    slot = ("lz", "lx")
    in_specs = (
        P(slot, None, "feat"),
        P(slot, None, "feat"),
        P(slot, "feat"),
        P(slot, None, "feat", None),
        P(None, "feat"),
        P(),
        P(None, slot, "feat"),
    )
    out_specs = (P(None, slot, "feat"), P(slot, None, "feat"))
    return jax.shard_map(local, mesh=split, in_specs=in_specs, out_specs=out_specs, check_vma=False)
```

```python
import jax
import jax.numpy as jnp
from jax import lax
from jax.sharding import Mesh
from jax.sharding import PartitionSpec as P

PLANE = ("lx", "feat")
EVERY = ("lz", "lx", "feat")


def bit_labels(axes):
    labels = []
    for axis in axes:
        size = lax.axis_size(axis)
        bits = size.bit_length() - 1
        assert 1 << bits == size
        labels += [(axis, b) for b in reversed(range(bits))]
    return labels


def plan(axes):
    labels = bit_labels(axes)
    prefix = [("feat", 0)]
    suffix = [("lz", lax.axis_size("lz").bit_length() - 2)] if "lz" in axes else []
    rotation = [label for label in labels if label not in prefix + suffix]
    orders = [rotation[p:] + rotation[:p] for p in range(len(rotation))]
    return labels, prefix, orders, suffix


def row_split(rows, parts):
    base = (rows // (8 * parts)) * 8
    sizes = [base] * parts
    extra = rows - base * parts
    i = 0
    while extra >= 8:
        sizes[i % parts] += 8
        extra -= 8
        i += 1
    sizes[0] += extra
    return sizes


def partner(axis, bit):
    return [(i, i ^ (1 << bit)) for i in range(lax.axis_size(axis))]


def portion_rows(rows, parts):
    sizes = row_split(rows, parts)
    return [(sum(sizes[:i]), sizes[i]) for i in range(parts)]


def reduce_scatter(blocks, axes, wire):
    labels, prefix, orders, suffix = plan(axes)
    n, rows, cols = blocks.shape
    nb = len(labels)
    x = blocks.reshape([2] * nb + [rows, cols])
    steps = [prefix + order + suffix for order in orders]
    parts = []
    for (start, size), order in zip(portion_rows(rows, len(orders)), steps):
        xp = lax.slice_in_dim(x, start, start + size, axis=nb)
        xp = jnp.transpose(xp, [labels.index(l) for l in order] + [nb, nb + 1])
        parts.append(xp.reshape(n, size, cols))
    for k in range(nb):
        for p in range(len(parts)):
            axis, bit = steps[p][k]
            own = (lax.axis_index(axis) >> bit) & 1
            half = parts[p].shape[0] // 2
            keep = lax.dynamic_slice_in_dim(parts[p], own * half, half, 0)
            send = lax.dynamic_slice_in_dim(parts[p], (1 - own) * half, half, 0)
            recv = lax.ppermute(send.astype(wire), axis, partner(axis, bit))
            parts[p] = keep + recv.astype(keep.dtype)
    return [xp[0] for xp in parts]


def split_rows(block, axes):
    _, _, orders, _ = plan(axes)
    return [lax.slice_in_dim(block, s, s + z, axis=0) for s, z in portion_rows(block.shape[0], len(orders))]


def all_gather(pieces, axes):
    labels, prefix, orders, suffix = plan(axes)
    rows = sum(p.shape[0] for p in pieces)
    cols = pieces[0].shape[1]
    nb = len(labels)
    steps = [prefix + order + suffix for order in orders]
    spans = portion_rows(rows, len(orders))
    parts = [p[None] for p in pieces]
    for k in reversed(range(nb)):
        for p in range(len(parts)):
            axis, bit = steps[p][k]
            own = (lax.axis_index(axis) >> bit) & 1
            recv = lax.ppermute(parts[p], axis, partner(axis, bit))
            parts[p] = jnp.where(
                own == 0, jnp.concatenate([parts[p], recv]), jnp.concatenate([recv, parts[p]])
            )
    out = []
    for xp, order, (start, size) in zip(parts, steps, spans):
        xp = xp.reshape([2] * nb + [size, cols])
        xp = jnp.transpose(xp, [order.index(l) for l in labels] + [nb, nb + 1])
        out.append(xp.reshape(-1, size, cols))
    return jnp.concatenate(out, axis=1)


def local(resid, encoder, encoder_bias, decoder, decoder_bias, topk_index, target):
    planes = lax.axis_size("lz")
    feat_parts = lax.axis_size("feat")
    layer_id = lax.axis_index("lz")
    half_bit = lax.axis_index("lx")
    feat_pos = lax.axis_index("feat")
    layer_count = decoder.shape[1]
    feat_dev = encoder.shape[2]
    half_rows = resid.shape[1]
    cols = resid.shape[2]
    tokens = 2 * half_rows
    width = cols * feat_parts
    slots = 2 * planes
    slot_rows = tokens // slots
    feat_total = 2 * feat_parts * feat_dev

    gathered = all_gather(split_rows(resid[0], PLANE), PLANE)
    tokens_all = (
        gathered.reshape(2, feat_parts, half_rows, cols).transpose(0, 2, 1, 3).reshape(tokens, width)
    )
    pre = jnp.dot(tokens_all, encoder[0], preferred_element_type=jnp.float32) + encoder_bias[0]
    first_feat = half_bit * (feat_total // 2) + feat_pos * feat_dev
    feat_ids = first_feat + lax.iota(jnp.int32, feat_dev)
    layer_index = lax.dynamic_index_in_dim(topk_index, layer_id, 0, keepdims=False)
    selected = jnp.any(layer_index[:, :, None] == feat_ids[None, None, :], axis=1).astype(
        jnp.float32
    )
    acts = (selected * pre).astype(jnp.bfloat16)
    live_layers = lax.iota(jnp.int32, layer_count) >= layer_id
    partial_value = jnp.einsum("tf,lfd->ltd", acts, decoder[0], preferred_element_type=jnp.float32)
    partial_value = jnp.where(live_layers[:, None, None], partial_value, 0.0)
    blocks = (
        partial_value.reshape(layer_count, slots, slot_rows, feat_parts, cols)
        .transpose(1, 3, 0, 2, 4)
        .reshape(slots * feat_parts, layer_count * slot_rows, cols)
    )
    recon_parts = reduce_scatter(blocks, EVERY, jnp.float32)
    bias_rows = jnp.broadcast_to(decoder_bias[:, None, :], target.shape).reshape(-1, cols)
    target_rows = target.reshape(-1, cols).astype(jnp.float32)
    error_parts = []
    start = 0
    for part in recon_parts:
        size = part.shape[0]
        bias_part = lax.slice_in_dim(bias_rows, start, start + size, axis=0)
        target_part = lax.slice_in_dim(target_rows, start, start + size, axis=0)
        error_parts.append((part + bias_part - target_part).astype(jnp.bfloat16))
        start += size
    error = jnp.concatenate(error_parts, axis=0).reshape(layer_count, slot_rows, cols)
    pieces = all_gather(error_parts, EVERY)
    piece = (
        pieces.reshape(slots, feat_parts, layer_count, slot_rows, cols)
        .transpose(2, 0, 3, 1, 4)
        .reshape(layer_count, tokens, width)
    )
    kept = jnp.where(live_layers[:, None, None], piece, jnp.zeros_like(piece))
    grad_act = jnp.einsum("ltd,lfd->tf", kept, decoder[0], preferred_element_type=jnp.float32)
    grad_pre = (selected * grad_act).astype(jnp.bfloat16)
    grad_part = lax.dot_general(
        grad_pre, encoder[0], (((1,), (1,)), ((), ())), preferred_element_type=jnp.float32
    )
    grad_blocks = (
        grad_part.reshape(2, half_rows, feat_parts, cols)
        .transpose(0, 2, 1, 3)
        .reshape(2 * feat_parts, half_rows, cols)
    )
    grad_sum = jnp.concatenate(reduce_scatter(grad_blocks, PLANE, jnp.float32), axis=0)
    return (error, grad_sum.astype(jnp.bfloat16)[None])


def solution(mesh):
    layer_n = mesh.shape["layer"]
    feat_n = mesh.shape["feat"]
    split = Mesh(mesh.devices.reshape(layer_n // 2, 2, feat_n), ("lz", "lx", "feat"))
    slot = ("lz", "lx")
    in_specs = (
        P(slot, None, "feat"),
        P(slot, None, "feat"),
        P(slot, "feat"),
        P(slot, None, "feat", None),
        P(None, "feat"),
        P(),
        P(None, slot, "feat"),
    )
    out_specs = (P(None, slot, "feat"), P(slot, None, "feat"))
    return jax.shard_map(local, mesh=split, in_specs=in_specs, out_specs=out_specs, check_vma=False)
```

```python
import jax
import jax.numpy as jnp
from jax import lax
from jax.sharding import Mesh
from jax.sharding import PartitionSpec as P

PLANE = ("lx", "feat")
EVERY = ("lz", "lx", "feat")


def bit_labels(axes):
    labels = []
    for axis in axes:
        size = lax.axis_size(axis)
        bits = size.bit_length() - 1
        assert 1 << bits == size
        labels += [(axis, b) for b in reversed(range(bits))]
    return labels


def plan(axes):
    labels = bit_labels(axes)
    prefix = [("feat", 0)]
    suffix = [("lz", lax.axis_size("lz").bit_length() - 2)] if "lz" in axes else []
    rotation = [label for label in labels if label not in prefix + suffix]
    orders = [rotation[p:] + rotation[:p] for p in range(len(rotation))]
    return labels, prefix, orders, suffix


def row_split(rows, parts):
    base = (rows // (8 * parts)) * 8
    sizes = [base] * parts
    extra = rows - base * parts
    i = 0
    while extra >= 8:
        sizes[i % parts] += 8
        extra -= 8
        i += 1
    sizes[0] += extra
    return sizes


def partner(axis, bit):
    return [(i, i ^ (1 << bit)) for i in range(lax.axis_size(axis))]


def portion_rows(rows, parts):
    sizes = row_split(rows, parts)
    return [(sum(sizes[:i]), sizes[i]) for i in range(parts)]


def halve(x, label, wire):
    axis, bit = label
    own = (lax.axis_index(axis) >> bit) & 1
    half = x.shape[0] // 2
    keep = lax.dynamic_slice_in_dim(x, own * half, half, 0)
    send = lax.dynamic_slice_in_dim(x, (1 - own) * half, half, 0)
    recv = lax.ppermute(send.astype(wire), axis, partner(axis, bit))
    return keep + recv.astype(keep.dtype)


def double(x, label):
    axis, bit = label
    own = (lax.axis_index(axis) >> bit) & 1
    recv = lax.ppermute(x, axis, partner(axis, bit))
    return jnp.where(own == 0, jnp.concatenate([x, recv]), jnp.concatenate([recv, x]))


def reduce_scatter(blocks, axes, wire):
    labels, prefix, orders, suffix = plan(axes)
    n, rows, cols = blocks.shape
    nb = len(labels)
    rest = [l for l in labels if l not in prefix]
    x = blocks.reshape([2] * nb + [rows, cols])
    x = jnp.transpose(x, [labels.index(l) for l in prefix + rest] + [nb, nb + 1])
    x = x.reshape(n, rows, cols)
    for label in prefix:
        x = halve(x, label, wire)
    x = x.reshape([2] * len(rest) + [rows, cols])
    parts = []
    for (start, size), order in zip(portion_rows(rows, len(orders)), orders):
        xp = lax.slice_in_dim(x, start, start + size, axis=len(rest))
        xp = jnp.transpose(xp, [rest.index(l) for l in order + suffix] + [len(rest), len(rest) + 1])
        parts.append(xp.reshape(-1, size, cols))
    for k in range(len(orders[0])):
        for p in range(len(parts)):
            parts[p] = halve(parts[p], orders[p][k], wire)
    x = jnp.concatenate(parts, axis=1)
    for label in suffix:
        x = halve(x, label, wire)
    return x[0]


def all_gather(block, axes):
    labels, prefix, orders, suffix = plan(axes)
    rows, cols = block.shape
    nb = len(labels)
    rest = [l for l in labels if l not in prefix]
    x = block[None]
    for label in reversed(suffix):
        x = double(x, label)
    spans = portion_rows(rows, len(orders))
    parts = [lax.slice_in_dim(x, start, start + size, axis=1) for start, size in spans]
    for k in reversed(range(len(orders[0]))):
        for p in range(len(parts)):
            parts[p] = double(parts[p], orders[p][k])
    out = []
    for xp, order, (start, size) in zip(parts, orders, spans):
        xp = xp.reshape([2] * len(rest) + [size, cols])
        have = order + suffix
        xp = jnp.transpose(xp, [have.index(l) for l in rest] + [len(rest), len(rest) + 1])
        out.append(xp.reshape(-1, size, cols))
    x = jnp.concatenate(out, axis=1)
    for label in reversed(prefix):
        x = double(x, label)
    x = x.reshape([2] * nb + [rows, cols])
    have = prefix + rest
    x = jnp.transpose(x, [have.index(l) for l in labels] + [nb, nb + 1])
    return x.reshape(-1, rows, cols)


def local(resid, encoder, encoder_bias, decoder, decoder_bias, topk_index, target):
    planes = lax.axis_size("lz")
    feat_parts = lax.axis_size("feat")
    layer_id = lax.axis_index("lz")
    half_bit = lax.axis_index("lx")
    feat_pos = lax.axis_index("feat")
    layer_count = decoder.shape[1]
    feat_dev = encoder.shape[2]
    half_rows = resid.shape[1]
    cols = resid.shape[2]
    tokens = 2 * half_rows
    width = cols * feat_parts
    slots = 2 * planes
    slot_rows = tokens // slots
    feat_total = 2 * feat_parts * feat_dev

    gathered = all_gather(resid[0], PLANE)
    tokens_all = (
        gathered.reshape(2, feat_parts, half_rows, cols).transpose(0, 2, 1, 3).reshape(tokens, width)
    )
    pre = jnp.dot(tokens_all, encoder[0], preferred_element_type=jnp.float32) + encoder_bias[0]
    first_feat = half_bit * (feat_total // 2) + feat_pos * feat_dev
    feat_ids = first_feat + lax.iota(jnp.int32, feat_dev)
    layer_index = lax.dynamic_index_in_dim(topk_index, layer_id, 0, keepdims=False)
    selected = jnp.any(layer_index[:, :, None] == feat_ids[None, None, :], axis=1).astype(
        jnp.float32
    )
    acts = (selected * pre).astype(jnp.bfloat16)
    live_layers = lax.iota(jnp.int32, layer_count) >= layer_id
    partial_value = jnp.einsum("tf,lfd->ltd", acts, decoder[0], preferred_element_type=jnp.float32)
    partial_value = jnp.where(live_layers[:, None, None], partial_value, 0.0)
    blocks = (
        partial_value.reshape(layer_count, slots, slot_rows, feat_parts, cols)
        .transpose(1, 3, 0, 2, 4)
        .reshape(slots * feat_parts, layer_count * slot_rows, cols)
    )
    recon = reduce_scatter(blocks, EVERY, jnp.float32).reshape(layer_count, slot_rows, cols)
    recon = recon + decoder_bias[:, None, :]
    error = (recon - target.astype(jnp.float32)).astype(jnp.bfloat16)
    pieces = all_gather(error.reshape(layer_count * slot_rows, cols), EVERY)
    piece = (
        pieces.reshape(slots, feat_parts, layer_count, slot_rows, cols)
        .transpose(2, 0, 3, 1, 4)
        .reshape(layer_count, tokens, width)
    )
    kept = jnp.where(live_layers[:, None, None], piece, jnp.zeros_like(piece))
    grad_act = jnp.einsum("ltd,lfd->tf", kept, decoder[0], preferred_element_type=jnp.float32)
    grad_pre = (selected * grad_act).astype(jnp.bfloat16)
    grad_part = lax.dot_general(
        grad_pre, encoder[0], (((1,), (1,)), ((), ())), preferred_element_type=jnp.float32
    )
    grad_blocks = (
        grad_part.reshape(2, half_rows, feat_parts, cols)
        .transpose(0, 2, 1, 3)
        .reshape(2 * feat_parts, half_rows, cols)
    )
    grad_sum = reduce_scatter(grad_blocks, PLANE, jnp.float32)
    return (error, grad_sum.astype(jnp.bfloat16)[None])


def solution(mesh):
    layer_n = mesh.shape["layer"]
    feat_n = mesh.shape["feat"]
    split = Mesh(mesh.devices.reshape(layer_n // 2, 2, feat_n), ("lz", "lx", "feat"))
    slot = ("lz", "lx")
    in_specs = (
        P(slot, None, "feat"),
        P(slot, None, "feat"),
        P(slot, "feat"),
        P(slot, None, "feat", None),
        P(None, "feat"),
        P(),
        P(None, slot, "feat"),
    )
    out_specs = (P(None, slot, "feat"), P(slot, None, "feat"))
    return jax.shard_map(local, mesh=split, in_specs=in_specs, out_specs=out_specs, check_vma=False)
```

```python
import jax
import jax.numpy as jnp
from jax import lax
from jax.sharding import Mesh
from jax.sharding import PartitionSpec as P

PLANE = ("lx", "feat")
EVERY = ("lz", "lx", "feat")


def bit_labels(axes):
    labels = []
    for axis in axes:
        size = lax.axis_size(axis)
        bits = size.bit_length() - 1
        assert 1 << bits == size
        labels += [(axis, b) for b in reversed(range(bits))]
    return labels


def plan(axes):
    labels = bit_labels(axes)
    prefix = [("feat", 0)]
    suffix = [("lz", lax.axis_size("lz").bit_length() - 2)] if "lz" in axes else []
    rotation = [label for label in labels if label not in prefix + suffix]
    orders = [rotation[p:] + rotation[:p] for p in range(len(rotation))]
    return labels, prefix, orders, suffix


def row_split(rows, parts):
    base = (rows // (8 * parts)) * 8
    sizes = [base] * parts
    extra = rows - base * parts
    i = 0
    while extra >= 8:
        sizes[i % parts] += 8
        extra -= 8
        i += 1
    sizes[0] += extra
    return sizes


def partner(axis, bit):
    return [(i, i ^ (1 << bit)) for i in range(lax.axis_size(axis))]


def portion_rows(rows, parts):
    sizes = row_split(rows, parts)
    return [(sum(sizes[:i]), sizes[i]) for i in range(parts)]


def reduce_scatter(blocks, axes, wire):
    labels, prefix, orders, suffix = plan(axes)
    n, rows, cols = blocks.shape
    nb = len(labels)
    x = blocks.reshape([2] * nb + [rows, cols])
    steps = [prefix + order + suffix for order in orders]
    parts = []
    for (start, size), order in zip(portion_rows(rows, len(orders)), steps):
        xp = lax.slice_in_dim(x, start, start + size, axis=nb)
        xp = jnp.transpose(xp, [labels.index(l) for l in order] + [nb, nb + 1])
        parts.append(xp.reshape(n, size, cols))
    for k in range(nb):
        for p in range(len(parts)):
            axis, bit = steps[p][k]
            own = (lax.axis_index(axis) >> bit) & 1
            half = parts[p].shape[0] // 2
            keep = lax.dynamic_slice_in_dim(parts[p], own * half, half, 0)
            send = lax.dynamic_slice_in_dim(parts[p], (1 - own) * half, half, 0)
            recv = lax.ppermute(send.astype(wire), axis, partner(axis, bit))
            parts[p] = keep + recv.astype(keep.dtype)
    return [xp[0] for xp in parts]


def split_rows(block, axes):
    _, _, orders, _ = plan(axes)
    return [lax.slice_in_dim(block, s, s + z, axis=0) for s, z in portion_rows(block.shape[0], len(orders))]


def all_gather(pieces, axes, companion=None):
    labels, prefix, orders, suffix = plan(axes)
    rows = sum(p.shape[0] for p in pieces)
    cols = pieces[0].shape[1]
    nb = len(labels)
    steps = [prefix + order + suffix for order in orders]
    spans = portion_rows(rows, len(orders))
    parts = [p[None] for p in pieces]
    for k in reversed(range(nb)):
        for p in range(len(parts)):
            axis, bit = steps[p][k]
            own = (lax.axis_index(axis) >> bit) & 1
            recv = lax.ppermute(parts[p], axis, partner(axis, bit))
            parts[p] = jnp.where(
                own == 0, jnp.concatenate([parts[p], recv]), jnp.concatenate([recv, parts[p]])
            )
        if companion is not None and k == nb - 1:
            parts, companion = lax.optimization_barrier((parts, companion))
    out = []
    for xp, order, (start, size) in zip(parts, steps, spans):
        xp = xp.reshape([2] * nb + [size, cols])
        xp = jnp.transpose(xp, [order.index(l) for l in labels] + [nb, nb + 1])
        out.append(xp.reshape(-1, size, cols))
    gathered = jnp.concatenate(out, axis=1)
    return gathered if companion is None else (gathered, companion)


def local(resid, encoder, encoder_bias, decoder, decoder_bias, topk_index, target):
    planes = lax.axis_size("lz")
    feat_parts = lax.axis_size("feat")
    layer_id = lax.axis_index("lz")
    half_bit = lax.axis_index("lx")
    feat_pos = lax.axis_index("feat")
    layer_count = decoder.shape[1]
    feat_dev = encoder.shape[2]
    half_rows = resid.shape[1]
    cols = resid.shape[2]
    tokens = 2 * half_rows
    width = cols * feat_parts
    slots = 2 * planes
    slot_rows = tokens // slots
    feat_total = 2 * feat_parts * feat_dev

    first_feat = half_bit * (feat_total // 2) + feat_pos * feat_dev
    feat_ids = first_feat + lax.iota(jnp.int32, feat_dev)
    layer_index = lax.dynamic_index_in_dim(topk_index, layer_id, 0, keepdims=False)
    selected = jnp.any(layer_index[:, :, None] == feat_ids[None, None, :], axis=1).astype(
        jnp.float32
    )
    gathered, selected = all_gather(split_rows(resid[0], PLANE), PLANE, selected)
    tokens_all = (
        gathered.reshape(2, feat_parts, half_rows, cols).transpose(0, 2, 1, 3).reshape(tokens, width)
    )
    pre = jnp.dot(tokens_all, encoder[0], preferred_element_type=jnp.float32) + encoder_bias[0]
    acts = (selected * pre).astype(jnp.bfloat16)
    live_layers = lax.iota(jnp.int32, layer_count) >= layer_id
    partial_value = jnp.einsum("tf,lfd->ltd", acts, decoder[0], preferred_element_type=jnp.float32)
    partial_value = jnp.where(live_layers[:, None, None], partial_value, 0.0)
    blocks = (
        partial_value.reshape(layer_count, slots, slot_rows, feat_parts, cols)
        .transpose(1, 3, 0, 2, 4)
        .reshape(slots * feat_parts, layer_count * slot_rows, cols)
    )
    recon_parts = reduce_scatter(blocks, EVERY, jnp.float32)
    bias_rows = jnp.broadcast_to(decoder_bias[:, None, :], target.shape).reshape(-1, cols)
    target_rows = target.reshape(-1, cols).astype(jnp.float32)
    error_parts = []
    start = 0
    for part in recon_parts:
        size = part.shape[0]
        bias_part = lax.slice_in_dim(bias_rows, start, start + size, axis=0)
        target_part = lax.slice_in_dim(target_rows, start, start + size, axis=0)
        error_parts.append((part + bias_part - target_part).astype(jnp.bfloat16))
        start += size
    error = jnp.concatenate(error_parts, axis=0).reshape(layer_count, slot_rows, cols)
    pieces = all_gather(error_parts, EVERY)
    piece = (
        pieces.reshape(slots, feat_parts, layer_count, slot_rows, cols)
        .transpose(2, 0, 3, 1, 4)
        .reshape(layer_count, tokens, width)
    )
    kept = jnp.where(live_layers[:, None, None], piece, jnp.zeros_like(piece))
    grad_act = jnp.einsum("ltd,lfd->tf", kept, decoder[0], preferred_element_type=jnp.float32)
    grad_pre = (selected * grad_act).astype(jnp.bfloat16)
    grad_part = lax.dot_general(
        grad_pre, encoder[0], (((1,), (1,)), ((), ())), preferred_element_type=jnp.float32
    )
    grad_blocks = (
        grad_part.reshape(2, half_rows, feat_parts, cols)
        .transpose(0, 2, 1, 3)
        .reshape(2 * feat_parts, half_rows, cols)
    )
    grad_sum = jnp.concatenate(reduce_scatter(grad_blocks, PLANE, jnp.float32), axis=0)
    return (error, grad_sum.astype(jnp.bfloat16)[None])


def solution(mesh):
    layer_n = mesh.shape["layer"]
    feat_n = mesh.shape["feat"]
    split = Mesh(mesh.devices.reshape(layer_n // 2, 2, feat_n), ("lz", "lx", "feat"))
    slot = ("lz", "lx")
    in_specs = (
        P(slot, None, "feat"),
        P(slot, None, "feat"),
        P(slot, "feat"),
        P(slot, None, "feat", None),
        P(None, "feat"),
        P(),
        P(None, slot, "feat"),
    )
    out_specs = (P(None, slot, "feat"), P(slot, None, "feat"))
    return jax.shard_map(local, mesh=split, in_specs=in_specs, out_specs=out_specs, check_vma=False)
```

```python
import jax
import jax.numpy as jnp
from jax import lax
from jax.sharding import Mesh
from jax.sharding import PartitionSpec as P

PLANE = ("lx", "feat")
EVERY = ("lz", "lx", "feat")


def bit_labels(axes):
    labels = []
    for axis in axes:
        size = lax.axis_size(axis)
        bits = size.bit_length() - 1
        assert 1 << bits == size
        labels += [(axis, b) for b in reversed(range(bits))]
    return labels


def plan(axes):
    labels = bit_labels(axes)
    prefix = [("feat", 0)]
    suffix = [("lz", lax.axis_size("lz").bit_length() - 2)] if "lz" in axes else []
    rotation = [label for label in labels if label not in prefix + suffix]
    orders = [rotation[p:] + rotation[:p] for p in range(min(2, len(rotation)))]
    return labels, prefix, orders, suffix


def row_split(rows, parts):
    base = (rows // (8 * parts)) * 8
    sizes = [base] * parts
    extra = rows - base * parts
    i = 0
    while extra >= 8:
        sizes[i % parts] += 8
        extra -= 8
        i += 1
    sizes[0] += extra
    return sizes


def partner(axis, bit):
    return [(i, i ^ (1 << bit)) for i in range(lax.axis_size(axis))]


def portion_rows(rows, parts):
    sizes = row_split(rows, parts)
    return [(sum(sizes[:i]), sizes[i]) for i in range(parts)]


def reduce_scatter(blocks, axes, wire):
    labels, prefix, orders, suffix = plan(axes)
    n, rows, cols = blocks.shape
    nb = len(labels)
    x = blocks.reshape([2] * nb + [rows, cols])
    steps = [prefix + order + suffix for order in orders]
    parts = []
    for (start, size), order in zip(portion_rows(rows, len(orders)), steps):
        xp = lax.slice_in_dim(x, start, start + size, axis=nb)
        xp = jnp.transpose(xp, [labels.index(l) for l in order] + [nb, nb + 1])
        parts.append(xp.reshape(n, size, cols))
    for k in range(nb):
        for p in range(len(parts)):
            axis, bit = steps[p][k]
            own = (lax.axis_index(axis) >> bit) & 1
            half = parts[p].shape[0] // 2
            keep = lax.dynamic_slice_in_dim(parts[p], own * half, half, 0)
            send = lax.dynamic_slice_in_dim(parts[p], (1 - own) * half, half, 0)
            recv = lax.ppermute(send.astype(wire), axis, partner(axis, bit))
            parts[p] = keep + recv.astype(keep.dtype)
    return [xp[0] for xp in parts]


def split_rows(block, axes):
    _, _, orders, _ = plan(axes)
    return [lax.slice_in_dim(block, s, s + z, axis=0) for s, z in portion_rows(block.shape[0], len(orders))]


def all_gather(pieces, axes):
    labels, prefix, orders, suffix = plan(axes)
    rows = sum(p.shape[0] for p in pieces)
    cols = pieces[0].shape[1]
    nb = len(labels)
    steps = [prefix + order + suffix for order in orders]
    spans = portion_rows(rows, len(orders))
    parts = [p[None] for p in pieces]
    for k in reversed(range(nb)):
        for p in range(len(parts)):
            axis, bit = steps[p][k]
            own = (lax.axis_index(axis) >> bit) & 1
            recv = lax.ppermute(parts[p], axis, partner(axis, bit))
            parts[p] = jnp.where(
                own == 0, jnp.concatenate([parts[p], recv]), jnp.concatenate([recv, parts[p]])
            )
    out = []
    for xp, order, (start, size) in zip(parts, steps, spans):
        xp = xp.reshape([2] * nb + [size, cols])
        xp = jnp.transpose(xp, [order.index(l) for l in labels] + [nb, nb + 1])
        out.append(xp.reshape(-1, size, cols))
    return jnp.concatenate(out, axis=1)


def local(resid, encoder, encoder_bias, decoder, decoder_bias, topk_index, target):
    planes = lax.axis_size("lz")
    feat_parts = lax.axis_size("feat")
    layer_id = lax.axis_index("lz")
    half_bit = lax.axis_index("lx")
    feat_pos = lax.axis_index("feat")
    layer_count = decoder.shape[1]
    feat_dev = encoder.shape[2]
    half_rows = resid.shape[1]
    cols = resid.shape[2]
    tokens = 2 * half_rows
    width = cols * feat_parts
    slots = 2 * planes
    slot_rows = tokens // slots
    feat_total = 2 * feat_parts * feat_dev

    gathered = all_gather(split_rows(resid[0], PLANE), PLANE)
    tokens_all = (
        gathered.reshape(2, feat_parts, half_rows, cols).transpose(0, 2, 1, 3).reshape(tokens, width)
    )
    pre = jnp.dot(tokens_all, encoder[0], preferred_element_type=jnp.float32) + encoder_bias[0]
    first_feat = half_bit * (feat_total // 2) + feat_pos * feat_dev
    feat_ids = first_feat + lax.iota(jnp.int32, feat_dev)
    layer_index = lax.dynamic_index_in_dim(topk_index, layer_id, 0, keepdims=False)
    selected = jnp.any(layer_index[:, :, None] == feat_ids[None, None, :], axis=1).astype(
        jnp.float32
    )
    acts = (selected * pre).astype(jnp.bfloat16)
    live_layers = lax.iota(jnp.int32, layer_count) >= layer_id
    partial_value = jnp.einsum("tf,lfd->ltd", acts, decoder[0], preferred_element_type=jnp.float32)
    partial_value = jnp.where(live_layers[:, None, None], partial_value, 0.0)
    blocks = (
        partial_value.reshape(layer_count, slots, slot_rows, feat_parts, cols)
        .transpose(1, 3, 0, 2, 4)
        .reshape(slots * feat_parts, layer_count * slot_rows, cols)
    )
    recon_parts = reduce_scatter(blocks, EVERY, jnp.float32)
    bias_rows = jnp.broadcast_to(decoder_bias[:, None, :], target.shape).reshape(-1, cols)
    target_rows = target.reshape(-1, cols).astype(jnp.float32)
    error_parts = []
    start = 0
    for part in recon_parts:
        size = part.shape[0]
        bias_part = lax.slice_in_dim(bias_rows, start, start + size, axis=0)
        target_part = lax.slice_in_dim(target_rows, start, start + size, axis=0)
        error_parts.append((part + bias_part - target_part).astype(jnp.bfloat16))
        start += size
    error = jnp.concatenate(error_parts, axis=0).reshape(layer_count, slot_rows, cols)
    pieces = all_gather(error_parts, EVERY)
    piece = (
        pieces.reshape(slots, feat_parts, layer_count, slot_rows, cols)
        .transpose(2, 0, 3, 1, 4)
        .reshape(layer_count, tokens, width)
    )
    kept = jnp.where(live_layers[:, None, None], piece, jnp.zeros_like(piece))
    grad_act = jnp.einsum("ltd,lfd->tf", kept, decoder[0], preferred_element_type=jnp.float32)
    grad_pre = (selected * grad_act).astype(jnp.bfloat16)
    grad_part = lax.dot_general(
        grad_pre, encoder[0], (((1,), (1,)), ((), ())), preferred_element_type=jnp.float32
    )
    grad_blocks = (
        grad_part.reshape(2, half_rows, feat_parts, cols)
        .transpose(0, 2, 1, 3)
        .reshape(2 * feat_parts, half_rows, cols)
    )
    grad_sum = jnp.concatenate(reduce_scatter(grad_blocks, PLANE, jnp.float32), axis=0)
    return (error, grad_sum.astype(jnp.bfloat16)[None])


def solution(mesh):
    layer_n = mesh.shape["layer"]
    feat_n = mesh.shape["feat"]
    split = Mesh(mesh.devices.reshape(layer_n // 2, 2, feat_n), ("lz", "lx", "feat"))
    slot = ("lz", "lx")
    in_specs = (
        P(slot, None, "feat"),
        P(slot, None, "feat"),
        P(slot, "feat"),
        P(slot, None, "feat", None),
        P(None, "feat"),
        P(),
        P(None, slot, "feat"),
    )
    out_specs = (P(None, slot, "feat"), P(slot, None, "feat"))
    return jax.shard_map(local, mesh=split, in_specs=in_specs, out_specs=out_specs, check_vma=False)
```

```python
import jax
import jax.numpy as jnp
from jax import lax
from jax.sharding import Mesh
from jax.sharding import PartitionSpec as P

PLANE = ("lx", "feat")
EVERY = ("lz", "lx", "feat")


def bit_labels(axes):
    labels = []
    for axis in axes:
        size = lax.axis_size(axis)
        bits = size.bit_length() - 1
        assert 1 << bits == size
        labels += [(axis, b) for b in reversed(range(bits))]
    return labels


def plan(axes):
    labels = bit_labels(axes)
    prefix = [("feat", 0)]
    suffix = [("lz", lax.axis_size("lz").bit_length() - 2)] if "lz" in axes else []
    rotation = [label for label in labels if label not in prefix + suffix]
    orders = [rotation[p:] + rotation[:p] for p in range(len(rotation))]
    return labels, prefix, orders, suffix


def row_split(rows, parts):
    base = (rows // (8 * parts)) * 8
    sizes = [base] * parts
    extra = rows - base * parts
    i = 0
    while extra >= 8:
        sizes[i % parts] += 8
        extra -= 8
        i += 1
    sizes[0] += extra
    return sizes


def partner(axis, bit):
    return [(i, i ^ (1 << bit)) for i in range(lax.axis_size(axis))]


def portion_rows(rows, parts):
    sizes = row_split(rows, parts)
    return [(sum(sizes[:i]), sizes[i]) for i in range(parts)]


def reduce_scatter(blocks, axes, wire):
    labels, prefix, orders, suffix = plan(axes)
    n, rows, cols = blocks.shape
    nb = len(labels)
    x = blocks.reshape([2] * nb + [rows, cols])
    steps = [prefix + order + suffix for order in orders]
    parts = []
    for (start, size), order in zip(portion_rows(rows, len(orders)), steps):
        xp = lax.slice_in_dim(x, start, start + size, axis=nb)
        xp = jnp.transpose(xp, [labels.index(l) for l in order] + [nb, nb + 1])
        parts.append(xp.reshape(n, size, cols))
    for k in range(nb):
        for p in range(len(parts)):
            axis, bit = steps[p][k]
            own = (lax.axis_index(axis) >> bit) & 1
            half = parts[p].shape[0] // 2
            keep = lax.dynamic_slice_in_dim(parts[p], own * half, half, 0)
            send = lax.dynamic_slice_in_dim(parts[p], (1 - own) * half, half, 0)
            recv = lax.ppermute(send.astype(wire), axis, partner(axis, bit))
            parts[p] = keep + recv.astype(keep.dtype)
    return [xp[0] for xp in parts]


def split_rows(block, axes):
    _, _, orders, _ = plan(axes)
    return [lax.slice_in_dim(block, s, s + z, axis=0) for s, z in portion_rows(block.shape[0], len(orders))]


def all_gather(pieces, axes):
    labels, prefix, orders, suffix = plan(axes)
    rows = sum(p.shape[0] for p in pieces)
    cols = pieces[0].shape[1]
    nb = len(labels)
    steps = [prefix + order + suffix for order in orders]
    spans = portion_rows(rows, len(orders))
    parts = [p[None] for p in pieces]
    for k in reversed(range(nb)):
        for p in range(len(parts)):
            axis, bit = steps[p][k]
            own = (lax.axis_index(axis) >> bit) & 1
            recv = lax.ppermute(parts[p], axis, partner(axis, bit))
            parts[p] = jnp.where(
                own == 0, jnp.concatenate([parts[p], recv]), jnp.concatenate([recv, parts[p]])
            )
    out = []
    for xp, order, (start, size) in zip(parts, steps, spans):
        xp = xp.reshape([2] * nb + [size, cols])
        xp = jnp.transpose(xp, [order.index(l) for l in labels] + [nb, nb + 1])
        out.append(xp.reshape(-1, size, cols))
    return jnp.concatenate(out, axis=1)


def local(resid, encoder, encoder_bias, decoder, decoder_bias, topk_index, target):
    planes = lax.axis_size("lz")
    feat_parts = lax.axis_size("feat")
    layer_id = lax.axis_index("lz")
    half_bit = lax.axis_index("lx")
    feat_pos = lax.axis_index("feat")
    layer_count = decoder.shape[1]
    feat_dev = encoder.shape[2]
    half_rows = resid.shape[1]
    cols = resid.shape[2]
    tokens = 2 * half_rows
    width = cols * feat_parts
    slots = 2 * planes
    slot_rows = tokens // slots
    feat_total = 2 * feat_parts * feat_dev

    gathered = all_gather(split_rows(resid[0], PLANE), PLANE)
    tokens_all = (
        gathered.reshape(2, feat_parts, half_rows, cols).transpose(0, 2, 1, 3).reshape(tokens, width)
    )
    pre = jnp.dot(tokens_all, encoder[0], preferred_element_type=jnp.float32) + encoder_bias[0]
    first_feat = half_bit * (feat_total // 2) + feat_pos * feat_dev
    layer_index = lax.dynamic_index_in_dim(topk_index, layer_id, 0, keepdims=False)
    local_ids = layer_index - first_feat
    low_bits = (feat_dev.bit_length() - 1) // 2
    side = 1 << low_bits
    high_hot = ((local_ids >> low_bits)[:, :, None] == lax.iota(jnp.int32, feat_dev // side)).astype(jnp.bfloat16)
    low_hot = ((local_ids & (side - 1))[:, :, None] == lax.iota(jnp.int32, side)).astype(jnp.bfloat16)
    selected = jnp.einsum("tka,tkb->tab", high_hot, low_hot, preferred_element_type=jnp.float32)
    selected = selected.reshape(tokens, feat_dev)
    acts = (selected * pre).astype(jnp.bfloat16)
    live_layers = lax.iota(jnp.int32, layer_count) >= layer_id
    partial_value = jnp.einsum("tf,lfd->ltd", acts, decoder[0], preferred_element_type=jnp.float32)
    partial_value = jnp.where(live_layers[:, None, None], partial_value, 0.0)
    blocks = (
        partial_value.reshape(layer_count, slots, slot_rows, feat_parts, cols)
        .transpose(1, 3, 0, 2, 4)
        .reshape(slots * feat_parts, layer_count * slot_rows, cols)
    )
    recon_parts = reduce_scatter(blocks, EVERY, jnp.float32)
    bias_rows = jnp.broadcast_to(decoder_bias[:, None, :], target.shape).reshape(-1, cols)
    target_rows = target.reshape(-1, cols).astype(jnp.float32)
    error_parts = []
    start = 0
    for part in recon_parts:
        size = part.shape[0]
        bias_part = lax.slice_in_dim(bias_rows, start, start + size, axis=0)
        target_part = lax.slice_in_dim(target_rows, start, start + size, axis=0)
        error_parts.append((part + bias_part - target_part).astype(jnp.bfloat16))
        start += size
    error = jnp.concatenate(error_parts, axis=0).reshape(layer_count, slot_rows, cols)
    pieces = all_gather(error_parts, EVERY)
    piece = (
        pieces.reshape(slots, feat_parts, layer_count, slot_rows, cols)
        .transpose(2, 0, 3, 1, 4)
        .reshape(layer_count, tokens, width)
    )
    kept = jnp.where(live_layers[:, None, None], piece, jnp.zeros_like(piece))
    grad_act = jnp.einsum("ltd,lfd->tf", kept, decoder[0], preferred_element_type=jnp.float32)
    grad_pre = (selected * grad_act).astype(jnp.bfloat16)
    grad_part = lax.dot_general(
        grad_pre, encoder[0], (((1,), (1,)), ((), ())), preferred_element_type=jnp.float32
    )
    grad_blocks = (
        grad_part.reshape(2, half_rows, feat_parts, cols)
        .transpose(0, 2, 1, 3)
        .reshape(2 * feat_parts, half_rows, cols)
    )
    grad_sum = jnp.concatenate(reduce_scatter(grad_blocks, PLANE, jnp.float32), axis=0)
    return (error, grad_sum.astype(jnp.bfloat16)[None])


def solution(mesh):
    layer_n = mesh.shape["layer"]
    feat_n = mesh.shape["feat"]
    split = Mesh(mesh.devices.reshape(layer_n // 2, 2, feat_n), ("lz", "lx", "feat"))
    slot = ("lz", "lx")
    in_specs = (
        P(slot, None, "feat"),
        P(slot, None, "feat"),
        P(slot, "feat"),
        P(slot, None, "feat", None),
        P(None, "feat"),
        P(),
        P(None, slot, "feat"),
    )
    out_specs = (P(None, slot, "feat"), P(slot, None, "feat"))
    return jax.shard_map(local, mesh=split, in_specs=in_specs, out_specs=out_specs, check_vma=False)
```

```python
import jax
import jax.numpy as jnp
from jax import lax
from jax.sharding import Mesh
from jax.sharding import PartitionSpec as P

PLANE = ("lx", "feat")
EVERY = ("lz", "lx", "feat")


def bit_labels(axes):
    labels = []
    for axis in axes:
        size = lax.axis_size(axis)
        bits = size.bit_length() - 1
        assert 1 << bits == size
        labels += [(axis, b) for b in reversed(range(bits))]
    return labels


def plan(axes):
    labels = bit_labels(axes)
    prefix = [("feat", 0)]
    suffix = [("lz", lax.axis_size("lz").bit_length() - 2)] if "lz" in axes else []
    rotation = [label for label in labels if label not in prefix + suffix]
    orders = [rotation[p:] + rotation[:p] for p in range(len(rotation))]
    return labels, prefix, orders, suffix


def row_split(rows, parts):
    base = (rows // (8 * parts)) * 8
    sizes = [base] * parts
    extra = rows - base * parts
    i = 0
    while extra >= 8:
        sizes[i % parts] += 8
        extra -= 8
        i += 1
    sizes[0] += extra
    return sizes


def partner(axis, bit):
    return [(i, i ^ (1 << bit)) for i in range(lax.axis_size(axis))]


def portion_rows(rows, parts):
    sizes = row_split(rows, parts)
    return [(sum(sizes[:i]), sizes[i]) for i in range(parts)]


def reduce_scatter(blocks, axes, wire):
    labels, prefix, orders, suffix = plan(axes)
    n, rows, cols = blocks.shape
    nb = len(labels)
    x = blocks.reshape([2] * nb + [rows, cols])
    steps = [prefix + order + suffix for order in orders]
    parts = []
    for (start, size), order in zip(portion_rows(rows, len(orders)), steps):
        xp = lax.slice_in_dim(x, start, start + size, axis=nb)
        xp = jnp.transpose(xp, [labels.index(l) for l in order] + [nb, nb + 1])
        parts.append(xp.reshape(n, size, cols))
    for k in range(nb):
        for p in range(len(parts)):
            axis, bit = steps[p][k]
            own = (lax.axis_index(axis) >> bit) & 1
            half = parts[p].shape[0] // 2
            keep = lax.dynamic_slice_in_dim(parts[p], own * half, half, 0)
            send = lax.dynamic_slice_in_dim(parts[p], (1 - own) * half, half, 0)
            recv = lax.ppermute(send.astype(wire), axis, partner(axis, bit))
            parts[p] = keep + recv.astype(keep.dtype)
    return [xp[0] for xp in parts]


def split_rows(block, axes):
    _, _, orders, _ = plan(axes)
    return [lax.slice_in_dim(block, s, s + z, axis=0) for s, z in portion_rows(block.shape[0], len(orders))]


def all_gather(pieces, axes):
    labels, prefix, orders, suffix = plan(axes)
    rows = sum(p.shape[0] for p in pieces)
    cols = pieces[0].shape[1]
    nb = len(labels)
    steps = [prefix + order + suffix for order in orders]
    spans = portion_rows(rows, len(orders))
    parts = [p[None] for p in pieces]
    for k in reversed(range(nb)):
        for p in range(len(parts)):
            axis, bit = steps[p][k]
            own = (lax.axis_index(axis) >> bit) & 1
            recv = lax.ppermute(parts[p], axis, partner(axis, bit))
            parts[p] = jnp.where(
                own == 0, jnp.concatenate([parts[p], recv]), jnp.concatenate([recv, parts[p]])
            )
    out = []
    for xp, order, (start, size) in zip(parts, steps, spans):
        xp = xp.reshape([2] * nb + [size, cols])
        xp = jnp.transpose(xp, [order.index(l) for l in labels] + [nb, nb + 1])
        out.append(xp.reshape(-1, size, cols))
    return jnp.concatenate(out, axis=1)


def local(resid, encoder, encoder_bias, decoder, decoder_bias, topk_index, target):
    planes = lax.axis_size("lz")
    feat_parts = lax.axis_size("feat")
    layer_id = lax.axis_index("lz")
    half_bit = lax.axis_index("lx")
    feat_pos = lax.axis_index("feat")
    layer_count = decoder.shape[1]
    feat_dev = encoder.shape[2]
    half_rows = resid.shape[1]
    cols = resid.shape[2]
    tokens = 2 * half_rows
    width = cols * feat_parts
    slots = 2 * planes
    slot_rows = tokens // slots
    feat_total = 2 * feat_parts * feat_dev

    gathered = all_gather(split_rows(resid[0], PLANE), PLANE)
    tokens_all = (
        gathered.reshape(2, feat_parts, half_rows, cols).transpose(0, 2, 1, 3).reshape(tokens, width)
    )
    pre = jnp.dot(tokens_all, encoder[0], preferred_element_type=jnp.float32) + encoder_bias[0]
    first_feat = half_bit * (feat_total // 2) + feat_pos * feat_dev
    layer_index = lax.dynamic_index_in_dim(topk_index, layer_id, 0, keepdims=False)
    local_ids = layer_index - first_feat
    low_bits = min(7, feat_dev.bit_length() - 1)
    side = 1 << low_bits
    high_hot = ((local_ids >> low_bits)[:, :, None] == lax.iota(jnp.int32, feat_dev // side)).astype(jnp.bfloat16)
    low_hot = ((local_ids & (side - 1))[:, :, None] == lax.iota(jnp.int32, side)).astype(jnp.bfloat16)
    selected = jnp.einsum("tka,tkb->tab", high_hot, low_hot, preferred_element_type=jnp.float32)
    selected = selected.reshape(tokens, feat_dev)
    acts = (selected * pre).astype(jnp.bfloat16)
    live_layers = lax.iota(jnp.int32, layer_count) >= layer_id
    partial_value = jnp.einsum("tf,lfd->ltd", acts, decoder[0], preferred_element_type=jnp.float32)
    partial_value = jnp.where(live_layers[:, None, None], partial_value, 0.0)
    blocks = (
        partial_value.reshape(layer_count, slots, slot_rows, feat_parts, cols)
        .transpose(1, 3, 0, 2, 4)
        .reshape(slots * feat_parts, layer_count * slot_rows, cols)
    )
    recon_parts = reduce_scatter(blocks, EVERY, jnp.float32)
    bias_rows = jnp.broadcast_to(decoder_bias[:, None, :], target.shape).reshape(-1, cols)
    target_rows = target.reshape(-1, cols).astype(jnp.float32)
    error_parts = []
    start = 0
    for part in recon_parts:
        size = part.shape[0]
        bias_part = lax.slice_in_dim(bias_rows, start, start + size, axis=0)
        target_part = lax.slice_in_dim(target_rows, start, start + size, axis=0)
        error_parts.append((part + bias_part - target_part).astype(jnp.bfloat16))
        start += size
    error = jnp.concatenate(error_parts, axis=0).reshape(layer_count, slot_rows, cols)
    pieces = all_gather(error_parts, EVERY)
    piece = (
        pieces.reshape(slots, feat_parts, layer_count, slot_rows, cols)
        .transpose(2, 0, 3, 1, 4)
        .reshape(layer_count, tokens, width)
    )
    kept = jnp.where(live_layers[:, None, None], piece, jnp.zeros_like(piece))
    grad_act = jnp.einsum("ltd,lfd->tf", kept, decoder[0], preferred_element_type=jnp.float32)
    grad_pre = (selected * grad_act).astype(jnp.bfloat16)
    grad_part = lax.dot_general(
        grad_pre, encoder[0], (((1,), (1,)), ((), ())), preferred_element_type=jnp.float32
    )
    grad_blocks = (
        grad_part.reshape(2, half_rows, feat_parts, cols)
        .transpose(0, 2, 1, 3)
        .reshape(2 * feat_parts, half_rows, cols)
    )
    grad_sum = jnp.concatenate(reduce_scatter(grad_blocks, PLANE, jnp.float32), axis=0)
    return (error, grad_sum.astype(jnp.bfloat16)[None])


def solution(mesh):
    layer_n = mesh.shape["layer"]
    feat_n = mesh.shape["feat"]
    split = Mesh(mesh.devices.reshape(layer_n // 2, 2, feat_n), ("lz", "lx", "feat"))
    slot = ("lz", "lx")
    in_specs = (
        P(slot, None, "feat"),
        P(slot, None, "feat"),
        P(slot, "feat"),
        P(slot, None, "feat", None),
        P(None, "feat"),
        P(),
        P(None, slot, "feat"),
    )
    out_specs = (P(None, slot, "feat"), P(slot, None, "feat"))
    return jax.shard_map(local, mesh=split, in_specs=in_specs, out_specs=out_specs, check_vma=False)
```

```python
import jax
import jax.numpy as jnp
from jax import lax
from jax.sharding import Mesh
from jax.sharding import PartitionSpec as P

PLANE = ("lx", "feat")
EVERY = ("lz", "lx", "feat")


def bit_labels(axes):
    labels = []
    for axis in axes:
        size = lax.axis_size(axis)
        bits = size.bit_length() - 1
        assert 1 << bits == size
        labels += [(axis, b) for b in reversed(range(bits))]
    return labels


def plan(axes):
    labels = bit_labels(axes)
    prefix = [("feat", 0)]
    suffix = [("lz", lax.axis_size("lz").bit_length() - 2)] if "lz" in axes else []
    rotation = [label for label in labels if label not in prefix + suffix]
    orders = [rotation[p:] + rotation[:p] for p in range(len(rotation))]
    return labels, prefix, orders, suffix


def row_split(rows, parts):
    base = (rows // (8 * parts)) * 8
    sizes = [base] * parts
    extra = rows - base * parts
    i = 0
    while extra >= 8:
        sizes[i % parts] += 8
        extra -= 8
        i += 1
    sizes[0] += extra
    return sizes


def partner(axis, bit):
    return [(i, i ^ (1 << bit)) for i in range(lax.axis_size(axis))]


def portion_rows(rows, parts):
    sizes = row_split(rows, parts)
    return [(sum(sizes[:i]), sizes[i]) for i in range(parts)]


def reduce_scatter(blocks, axes, wire):
    labels, prefix, orders, suffix = plan(axes)
    n, rows, cols = blocks.shape
    nb = len(labels)
    x = blocks.reshape([2] * nb + [rows, cols])
    steps = [prefix + order + suffix for order in orders]
    parts = []
    for (start, size), order in zip(portion_rows(rows, len(orders)), steps):
        xp = lax.slice_in_dim(x, start, start + size, axis=nb)
        xp = jnp.transpose(xp, [labels.index(l) for l in order] + [nb, nb + 1])
        parts.append(xp.reshape(n, size, cols))
    for k in range(nb):
        for p in range(len(parts)):
            axis, bit = steps[p][k]
            own = (lax.axis_index(axis) >> bit) & 1
            half = parts[p].shape[0] // 2
            keep = lax.dynamic_slice_in_dim(parts[p], own * half, half, 0)
            send = lax.dynamic_slice_in_dim(parts[p], (1 - own) * half, half, 0)
            recv = lax.ppermute(send.astype(wire), axis, partner(axis, bit))
            parts[p] = keep + recv.astype(keep.dtype)
    return [xp[0] for xp in parts]


def split_rows(block, axes):
    _, _, orders, _ = plan(axes)
    return [lax.slice_in_dim(block, s, s + z, axis=0) for s, z in portion_rows(block.shape[0], len(orders))]


def all_gather(pieces, axes):
    labels, prefix, orders, suffix = plan(axes)
    rows = sum(p.shape[0] for p in pieces)
    cols = pieces[0].shape[1]
    nb = len(labels)
    steps = [prefix + order + suffix for order in orders]
    spans = portion_rows(rows, len(orders))
    parts = [p[None] for p in pieces]
    for k in reversed(range(nb)):
        for p in range(len(parts)):
            axis, bit = steps[p][k]
            own = (lax.axis_index(axis) >> bit) & 1
            recv = lax.ppermute(parts[p], axis, partner(axis, bit))
            parts[p] = jnp.where(
                own == 0, jnp.concatenate([parts[p], recv]), jnp.concatenate([recv, parts[p]])
            )
    out = []
    for xp, order, (start, size) in zip(parts, steps, spans):
        xp = xp.reshape([2] * nb + [size, cols])
        xp = jnp.transpose(xp, [order.index(l) for l in labels] + [nb, nb + 1])
        out.append(xp.reshape(-1, size, cols))
    return jnp.concatenate(out, axis=1)


def local(resid, encoder, encoder_bias, decoder, decoder_bias, topk_index, target):
    planes = lax.axis_size("lz")
    feat_parts = lax.axis_size("feat")
    layer_id = lax.axis_index("lz")
    half_bit = lax.axis_index("lx")
    feat_pos = lax.axis_index("feat")
    layer_count = decoder.shape[1]
    feat_dev = encoder.shape[2]
    half_rows = resid.shape[1]
    cols = resid.shape[2]
    tokens = 2 * half_rows
    width = cols * feat_parts
    slots = 2 * planes
    slot_rows = tokens // slots
    feat_total = 2 * feat_parts * feat_dev

    gathered = all_gather(split_rows(resid[0], PLANE), PLANE)
    tokens_all = (
        gathered.reshape(2, feat_parts, half_rows, cols).transpose(0, 2, 1, 3).reshape(tokens, width)
    )
    pre = jnp.dot(tokens_all, encoder[0], preferred_element_type=jnp.float32) + encoder_bias[0]
    first_feat = half_bit * (feat_total // 2) + feat_pos * feat_dev
    layer_index = lax.dynamic_index_in_dim(topk_index, layer_id, 0, keepdims=False)
    local_ids = layer_index - first_feat
    low_bits = min(7, feat_dev.bit_length() - 1)
    side = 1 << low_bits
    high_hot = ((local_ids >> low_bits)[:, :, None] == lax.iota(jnp.int32, feat_dev // side)).astype(jnp.bfloat16)
    low_hot = ((local_ids & (side - 1))[:, :, None] == lax.iota(jnp.int32, side)).astype(jnp.bfloat16)
    selected = jnp.einsum("tka,tkb->tab", high_hot, low_hot, preferred_element_type=jnp.float32)
    selected = selected.astype(jnp.bfloat16)
    selected = selected.reshape(tokens, feat_dev)
    acts = (selected.astype(jnp.float32) * pre).astype(jnp.bfloat16)
    live_layers = lax.iota(jnp.int32, layer_count) >= layer_id
    partial_value = jnp.einsum("tf,lfd->ltd", acts, decoder[0], preferred_element_type=jnp.float32)
    partial_value = jnp.where(live_layers[:, None, None], partial_value, 0.0)
    blocks = (
        partial_value.reshape(layer_count, slots, slot_rows, feat_parts, cols)
        .transpose(1, 3, 0, 2, 4)
        .reshape(slots * feat_parts, layer_count * slot_rows, cols)
    )
    recon_parts = reduce_scatter(blocks, EVERY, jnp.float32)
    bias_rows = jnp.broadcast_to(decoder_bias[:, None, :], target.shape).reshape(-1, cols)
    target_rows = target.reshape(-1, cols).astype(jnp.float32)
    error_parts = []
    start = 0
    for part in recon_parts:
        size = part.shape[0]
        bias_part = lax.slice_in_dim(bias_rows, start, start + size, axis=0)
        target_part = lax.slice_in_dim(target_rows, start, start + size, axis=0)
        error_parts.append((part + bias_part - target_part).astype(jnp.bfloat16))
        start += size
    error = jnp.concatenate(error_parts, axis=0).reshape(layer_count, slot_rows, cols)
    pieces = all_gather(error_parts, EVERY)
    piece = (
        pieces.reshape(slots, feat_parts, layer_count, slot_rows, cols)
        .transpose(2, 0, 3, 1, 4)
        .reshape(layer_count, tokens, width)
    )
    kept = jnp.where(live_layers[:, None, None], piece, jnp.zeros_like(piece))
    grad_act = jnp.einsum("ltd,lfd->tf", kept, decoder[0], preferred_element_type=jnp.float32)
    grad_pre = (selected.astype(jnp.float32) * grad_act).astype(jnp.bfloat16)
    grad_part = lax.dot_general(
        grad_pre, encoder[0], (((1,), (1,)), ((), ())), preferred_element_type=jnp.float32
    )
    grad_blocks = (
        grad_part.reshape(2, half_rows, feat_parts, cols)
        .transpose(0, 2, 1, 3)
        .reshape(2 * feat_parts, half_rows, cols)
    )
    grad_sum = jnp.concatenate(reduce_scatter(grad_blocks, PLANE, jnp.float32), axis=0)
    return (error, grad_sum.astype(jnp.bfloat16)[None])


def solution(mesh):
    layer_n = mesh.shape["layer"]
    feat_n = mesh.shape["feat"]
    split = Mesh(mesh.devices.reshape(layer_n // 2, 2, feat_n), ("lz", "lx", "feat"))
    slot = ("lz", "lx")
    in_specs = (
        P(slot, None, "feat"),
        P(slot, None, "feat"),
        P(slot, "feat"),
        P(slot, None, "feat", None),
        P(None, "feat"),
        P(),
        P(None, slot, "feat"),
    )
    out_specs = (P(None, slot, "feat"), P(slot, None, "feat"))
    return jax.shard_map(local, mesh=split, in_specs=in_specs, out_specs=out_specs, check_vma=False)
```
